128 devices in a mesh: grp: 8 (over x_hi, y), seq: 16 (over x_lo, z, core).
Axes of the slice: x: 4 (x_hi: 2, x_lo: 2; x = x_hi * 2 + x_lo), y: 4, z: 4, core: 2. Of those that a mesh axis runs over, the one named last changes fastest.
Arguments:
- clip_latents: bfloat16 [8, 32, 16, 7680], P('grp', 'seq'), may hold values from -6 to 6
- adjoint_seed: bfloat16 [8, 32, 16, 7680], P('grp', 'seq'), may hold values from -6 to 6
- kernel_matrix: bfloat16 [2880, 320], replicated, may hold values from -0.109375 to 0.109375
- triple_projector: bfloat16 [320, 960], replicated, may hold values from -0.3125 to 0.3125
- exit_projector: bfloat16 [320, 320], replicated, may hold values from -0.3125 to 0.3125
- logit_scaling: float32 [5], replicated, may hold values from 4 to 24
Outputs:
- output: bfloat16 [8, 32, 16, 7680], P('grp', 'seq')
- d_video: bfloat16 [8, 32, 16, 7680], P('grp', 'seq')
- g_conv: float32 [2880, 320], replicated
- g_qkv: float32 [320, 960], replicated
- g_out: float32 [320, 320], replicated
The draws below stay inside these ranges and needn't reach their ends.
All inputs are finite; a program needn't handle non-finite values.
Results may differ from the reference program's by a relative error of at most 0.019.
Values may be sent and summed in bfloat16 or wider, within the bound.
No kernel may reach another device: no remote copies, remote signals or barrier semaphores. Data moves between devices by JAX's collectives and lax.ppermute only.
A program may use at most 128 MiB of HBM per device.

```python
import math
import jax
import jax.numpy as jnp
from jax import lax

C = 320
HEAD_DIM = 64
GROUPS = 32
HEAD_NUMBER = 5
HH = 16
WW = 24
FRAMES = 32
VIDEOS = 8


def block_scale(rng, dims, cuts, low, largest):
    def one(dim, parts):
        heights = jax.random.uniform(jax.random.fold_in(jax.random.fold_in(rng, 6), dim), (parts,), jnp.float32, low / len(cuts), largest / len(cuts))
        return jnp.repeat(jnp.exp(heights), dims[dim] // parts).reshape((-1,) + (1,) * (len(dims) - dim - 1))

    level = one(*cuts[0])
    for cut in cuts[1:]:
        level = level * one(*cut)
    return level


def centred(own_key, dims, scale, reach, shards=(), dtype=jnp.bfloat16):
    result = jax.random.normal(own_key, dims, jnp.float32) * scale
    if len(shards) > 0:
        result = block_scale(own_key, dims, shards, -0.22, 0.18) * result
    return jnp.clip(result, min=-reach, max=reach).astype(dtype)


def setup_inputs(seed: int = 0) -> dict:
    seeds = jax.random.split(jax.random.key(seed), 7)
    return {
        "clip_latents": centred(seeds[0], (VIDEOS, FRAMES, HH, WW * C), 1.0, 6.0, ((0, 8), (1, 16))),
        "adjoint_seed": centred(seeds[1], (VIDEOS, FRAMES, HH, WW * C), 1.0, 6.0, ((0, 8), (1, 16))),
        "kernel_matrix": centred(seeds[2], (9 * C, C), (9 * C) ** -0.5, 0.109375),
        "triple_projector": centred(seeds[3], (C, 3 * C), C ** -0.5, 0.3125),
        "exit_projector": centred(seeds[4], (C, C), C ** -0.5, 0.3125),
        "logit_scaling": jnp.clip(jnp.exp(jax.random.uniform(seeds[5], (HEAD_NUMBER,), jnp.float32, math.log(4.0), math.log(24.0))), 4.0, 24.0),
    }


def group_act(widened):
    frames, height, breadth, channels = widened.shape
    grouped = widened.reshape(frames, height * breadth, GROUPS, channels // GROUPS)
    centre = lax.optimization_barrier(jnp.mean(grouped, axis=(1, 3), keepdims=True))
    spread = lax.optimization_barrier(jnp.mean(jnp.square(grouped - centre), axis=(1, 3), keepdims=True))
    normed = (grouped - centre) * lax.rsqrt(spread + 1e-05)
    return jax.nn.silu(normed).reshape(frames, height, breadth, channels)

def make_patches(active):
    frames, height, breadth, channels = active.shape
    padded = jnp.pad(active, ((0, 0), (1, 1), (1, 1), (0, 0)))
    pieces = [padded[:, down_step:down_step + height, side_step:side_step + breadth, :] for down_step in range(3) for side_step in range(3)]
    return jnp.concatenate(pieces, axis=-1).reshape(frames * height * breadth, 9 * channels)

def fold_patches(columns, frames, height, breadth):
    channels = columns.shape[-1] // 9
    pieces = columns.reshape(frames, height, breadth, 9, channels)
    totals = jnp.zeros((frames, height + 2, breadth + 2, channels), jnp.float32)
    for down_step in range(3):
        for side_step in range(3):
            shifted = pieces[:, :, :, down_step * 3 + side_step, :]
            totals = totals + jnp.pad(shifted, ((0, 0), (down_step, 2 - down_step), (side_step, 2 - side_step), (0, 0)))
    return totals[:, 1:height + 1, 1:breadth + 1, :]

def layer_norm(widened):
    centre = lax.optimization_barrier(jnp.mean(widened, axis=-1, keepdims=True))
    spread = lax.optimization_barrier(jnp.mean(jnp.square(widened - centre), axis=-1, keepdims=True))
    return (widened - centre) * lax.rsqrt(spread + 1e-05)

def temporal_mixing(mapped_tokens, logit_scaling):
    frames, places, triple = mapped_tokens.shape
    channels = triple // 3
    head_count = channels // HEAD_DIM
    pieces = mapped_tokens.reshape(frames, places, 3, head_count, HEAD_DIM)
    probe_tokens = pieces[:, :, 0]
    keyset = pieces[:, :, 1]
    valueset = pieces[:, :, 2].astype(jnp.bfloat16)
    probe_tokens = (probe_tokens * lax.rsqrt(lax.optimization_barrier(jnp.sum(probe_tokens * probe_tokens, axis=-1, keepdims=True)) + 1e-06) * logit_scaling[:, None]).astype(jnp.bfloat16)
    keyset = (keyset * lax.rsqrt(lax.optimization_barrier(jnp.sum(keyset * keyset, axis=-1, keepdims=True)) + 1e-06)).astype(jnp.bfloat16)
    scores = jnp.einsum('flhd,glhd->lhfg', probe_tokens.astype(jnp.float32), keyset.astype(jnp.float32))
    weights = jnp.exp(scores)
    weights = (weights / lax.optimization_barrier(jnp.sum(weights, axis=-1, keepdims=True))).astype(jnp.bfloat16)
    softmax_blend = jnp.einsum('lhfg,glhd->flhd', weights.astype(jnp.float32), valueset.astype(jnp.float32))
    return softmax_blend.reshape(frames, places, channels)

def contract_rows(left, right):
    return lax.dot_general(left, right, (((0,), (0,)), ((), ())), preferred_element_type=jnp.float32)

def spatial_forward(source, kernel_matrix):
    frames, height, breadth, channels = source.shape
    widened = source.astype(jnp.float32)
    active, pull_act = jax.vjp(group_act, widened)
    patches = make_patches(active.astype(jnp.bfloat16))
    convolved = jnp.dot(patches, kernel_matrix, preferred_element_type=jnp.float32)
    latent_features = (widened.reshape(frames * height * breadth, channels) + convolved).astype(jnp.bfloat16)
    return (latent_features, patches, pull_act)

def spatial_backward(upstream_adjoint, patches, pull_act, kernel_matrix, frames, height, breadth):
    channels = upstream_adjoint.shape[-1]
    grad_conv = contract_rows(patches, upstream_adjoint)
    columns = jnp.dot(upstream_adjoint, kernel_matrix.T, preferred_element_type=jnp.float32)
    d_active = fold_patches(columns, frames, height, breadth)
    d_source = pull_act(d_active)[0]
    section_outcome = (upstream_adjoint.astype(jnp.float32).reshape(frames, height, breadth, channels) + d_source).astype(jnp.bfloat16)
    return (section_outcome, grad_conv)

def temporal_mixing_apply(latent_features, triple_projector, exit_projector, logit_scaling):
    frames, places, channels = latent_features.shape
    widened = latent_features.astype(jnp.float32)
    standardised_tokens = layer_norm(widened).astype(jnp.bfloat16)
    mapped_tokens = jnp.dot(standardised_tokens.reshape(frames * places, channels), triple_projector, preferred_element_type=jnp.float32).reshape(frames, places, 3 * channels)
    softmax_blend = temporal_mixing(mapped_tokens, logit_scaling).astype(jnp.bfloat16)
    branch = jnp.dot(softmax_blend.reshape(frames * places, channels), exit_projector, preferred_element_type=jnp.float32)
    section_outcome = (widened + branch.reshape(frames, places, channels)).astype(jnp.bfloat16)
    return (section_outcome, standardised_tokens, mapped_tokens, softmax_blend)

def temporal_mixing_reverse(latent_features, upstream_adjoint, standardised_tokens, mapped_tokens, softmax_blend, triple_projector, exit_projector, logit_scaling):
    frames, places, channels = latent_features.shape
    rows_cot = upstream_adjoint.reshape(frames * places, channels)
    emitted_adjoint = contract_rows(softmax_blend.reshape(frames * places, channels), rows_cot)
    d_mixture = jnp.dot(rows_cot, exit_projector.T, preferred_element_type=jnp.float32).astype(jnp.bfloat16)
    discarded_item, temporal_mixing_adjoint = jax.vjp(lambda entry_tensor: temporal_mixing(entry_tensor, logit_scaling), mapped_tokens)
    d_projected = temporal_mixing_adjoint(d_mixture.astype(jnp.float32).reshape(frames, places, channels))[0].astype(jnp.bfloat16)
    rows_proj = d_projected.reshape(frames * places, 3 * channels)
    triple_projector_adjoint = contract_rows(standardised_tokens.reshape(frames * places, channels), rows_proj)
    d_normed = jnp.dot(rows_proj, triple_projector.T, preferred_element_type=jnp.float32).reshape(frames, places, channels)
    discarded_item, pull_norm = jax.vjp(layer_norm, latent_features.astype(jnp.float32))
    d_layer = pull_norm(d_normed)[0].astype(jnp.bfloat16)
    feature_adjoint = (upstream_adjoint.astype(jnp.float32) + d_layer.astype(jnp.float32)).astype(jnp.bfloat16)
    return (feature_adjoint, triple_projector_adjoint, emitted_adjoint)

def reference(clip_latents, adjoint_seed, kernel_matrix, triple_projector, exit_projector, logit_scaling):
    outputs = []
    d_inputs = []
    sum_conv = jnp.zeros((9 * C, C), jnp.float32)
    sum_qkv = jnp.zeros((C, 3 * C), jnp.float32)
    sum_out = jnp.zeros((C, C), jnp.float32)
    for sample in range(VIDEOS):
        source = clip_latents[sample].reshape(FRAMES, HH, WW, C)
        latent_features, patches, pull_act = spatial_forward(source, kernel_matrix)
        latent_features = latent_features.reshape(FRAMES, HH * WW, C)
        section_outcome, standardised_tokens, mapped_tokens, softmax_blend = temporal_mixing_apply(latent_features, triple_projector, exit_projector, logit_scaling)
        outputs.append(section_outcome.reshape(FRAMES, HH, WW * C))
        upstream_adjoint = adjoint_seed[sample].reshape(FRAMES, HH * WW, C)
        feature_adjoint, triple_projector_adjoint, emitted_adjoint = temporal_mixing_reverse(latent_features, upstream_adjoint, standardised_tokens, mapped_tokens, softmax_blend, triple_projector, exit_projector, logit_scaling)
        d_source, grad_conv = spatial_backward(feature_adjoint.reshape(FRAMES * HH * WW, C), patches, pull_act, kernel_matrix, FRAMES, HH, WW)
        d_inputs.append(d_source.reshape(FRAMES, HH, WW * C))
        sum_conv = sum_conv + grad_conv
        sum_qkv = sum_qkv + triple_projector_adjoint
        sum_out = sum_out + emitted_adjoint
    factor = 1.0 / math.sqrt(VIDEOS * FRAMES * HH * WW)
    return (jnp.stack(outputs), jnp.stack(d_inputs), sum_conv * factor, sum_qkv * factor, sum_out * factor)
```

```python
import math

import jax
import jax.numpy as jnp
from jax import lax
from jax.sharding import PartitionSpec as P

HEAD_DIM = 64
GROUPS = 32


def group_act(widened):
    frames, height, breadth, channels = widened.shape
    grouped = widened.reshape(frames, height * breadth, GROUPS, channels // GROUPS)
    centre = jnp.mean(grouped, axis=(1, 3), keepdims=True)
    spread = jnp.mean(jnp.square(grouped - centre), axis=(1, 3), keepdims=True)
    normed = (grouped - centre) * lax.rsqrt(spread + 1e-05)
    return jax.nn.silu(normed).reshape(frames, height, breadth, channels)


def make_patches(active):
    frames, height, breadth, channels = active.shape
    padded = jnp.pad(active, ((0, 0), (1, 1), (1, 1), (0, 0)))
    pieces = [
        padded[:, down_step : down_step + height, side_step : side_step + breadth, :]
        for down_step in range(3)
        for side_step in range(3)
    ]
    return jnp.concatenate(pieces, axis=-1).reshape(frames * height * breadth, 9 * channels)


def fold_patches(columns, frames, height, breadth):
    channels = columns.shape[-1] // 9
    pieces = columns.reshape(frames, height, breadth, 9, channels)
    totals = jnp.zeros((frames, height + 2, breadth + 2, channels), jnp.float32)
    for down_step in range(3):
        for side_step in range(3):
            shifted = pieces[:, :, :, down_step * 3 + side_step, :]
            totals = totals + jnp.pad(
                shifted, ((0, 0), (down_step, 2 - down_step), (side_step, 2 - side_step), (0, 0))
            )
    return totals[:, 1 : height + 1, 1 : breadth + 1, :]


def layer_norm(widened):
    centre = jnp.mean(widened, axis=-1, keepdims=True)
    spread = jnp.mean(jnp.square(widened - centre), axis=-1, keepdims=True)
    return (widened - centre) * lax.rsqrt(spread + 1e-05)


def head_mixing(query, keys, values, scaling):
    query = (
        query * lax.rsqrt(jnp.sum(query * query, axis=-1, keepdims=True) + 1e-06) * scaling
    ).astype(jnp.bfloat16)
    keys = (keys * lax.rsqrt(jnp.sum(keys * keys, axis=-1, keepdims=True) + 1e-06)).astype(
        jnp.bfloat16
    )
    values = values.astype(jnp.bfloat16)
    scores = jnp.einsum("fld,gld->lfg", query, keys, preferred_element_type=jnp.float32)
    weights = jnp.exp(scores)
    weights = (weights / jnp.sum(weights, axis=-1, keepdims=True)).astype(jnp.bfloat16)
    return jnp.einsum("lfg,gld->fld", weights, values, preferred_element_type=jnp.float32)


def temporal_mixing(mapped_tokens, logit_scaling):
    frames, places, triple = mapped_tokens.shape
    channels = triple // 3
    head_count = channels // HEAD_DIM
    blends = []
    for head in range(head_count):
        low = head * HEAD_DIM
        blends.append(
            head_mixing(
                mapped_tokens[:, :, low : low + HEAD_DIM],
                mapped_tokens[:, :, channels + low : channels + low + HEAD_DIM],
                mapped_tokens[:, :, 2 * channels + low : 2 * channels + low + HEAD_DIM],
                logit_scaling[head],
            )
        )
    return jnp.concatenate(blends, axis=-1)


def contract_rows(left, right):
    return lax.dot_general(
        left, right, (((0,), (0,)), ((), ())), preferred_element_type=jnp.float32
    )


def spatial_forward(source, kernel_matrix):
    frames, height, breadth, channels = source.shape
    widened = source.astype(jnp.float32)
    active, pull_act = jax.vjp(group_act, widened)
    patches = make_patches(active.astype(jnp.bfloat16))
    convolved = jnp.dot(patches, kernel_matrix, preferred_element_type=jnp.float32)
    latent_features = (widened.reshape(frames * height * breadth, channels) + convolved).astype(
        jnp.bfloat16
    )
    return (latent_features, patches, pull_act)


def spatial_backward(upstream_adjoint, patches, pull_act, kernel_matrix, frames, height, breadth):
    channels = upstream_adjoint.shape[-1]
    grad_conv = contract_rows(patches, upstream_adjoint)
    columns = jnp.dot(upstream_adjoint, kernel_matrix.T, preferred_element_type=jnp.float32)
    d_active = fold_patches(columns, frames, height, breadth)
    d_source = pull_act(d_active)[0]
    section_outcome = (
        upstream_adjoint.astype(jnp.float32).reshape(frames, height, breadth, channels) + d_source
    ).astype(jnp.bfloat16)
    return (section_outcome, grad_conv)


def temporal_mixing_apply(latent_features, triple_projector, exit_projector, logit_scaling):
    frames, places, channels = latent_features.shape
    widened = latent_features.astype(jnp.float32)
    standardised_tokens = layer_norm(widened).astype(jnp.bfloat16)
    mapped_tokens = jnp.dot(
        standardised_tokens.reshape(frames * places, channels),
        triple_projector,
        preferred_element_type=jnp.float32,
    ).reshape(frames, places, 3 * channels)
    softmax_blend = temporal_mixing(mapped_tokens, logit_scaling).astype(jnp.bfloat16)
    branch = jnp.dot(
        softmax_blend.reshape(frames * places, channels),
        exit_projector,
        preferred_element_type=jnp.float32,
    )
    section_outcome = (widened + branch.reshape(frames, places, channels)).astype(jnp.bfloat16)
    return (section_outcome, standardised_tokens, mapped_tokens, softmax_blend)


def temporal_mixing_reverse(
    latent_features,
    upstream_adjoint,
    standardised_tokens,
    mapped_tokens,
    softmax_blend,
    triple_projector,
    exit_projector,
    logit_scaling,
):
    frames, places, channels = latent_features.shape
    rows_cot = upstream_adjoint.reshape(frames * places, channels)
    emitted_adjoint = contract_rows(softmax_blend.reshape(frames * places, channels), rows_cot)
    d_mixture = jnp.dot(rows_cot, exit_projector.T, preferred_element_type=jnp.float32).astype(
        jnp.bfloat16
    )
    discarded_item, temporal_mixing_adjoint = jax.vjp(
        lambda entry_tensor: temporal_mixing(entry_tensor, logit_scaling), mapped_tokens
    )
    d_projected = temporal_mixing_adjoint(
        d_mixture.astype(jnp.float32).reshape(frames, places, channels)
    )[0].astype(jnp.bfloat16)
    rows_proj = d_projected.reshape(frames * places, 3 * channels)
    triple_projector_adjoint = contract_rows(
        standardised_tokens.reshape(frames * places, channels), rows_proj
    )
    d_normed = jnp.dot(rows_proj, triple_projector.T, preferred_element_type=jnp.float32).reshape(
        frames, places, channels
    )
    discarded_item, pull_norm = jax.vjp(layer_norm, latent_features.astype(jnp.float32))
    d_layer = pull_norm(d_normed)[0].astype(jnp.bfloat16)
    feature_adjoint = (upstream_adjoint.astype(jnp.float32) + d_layer.astype(jnp.float32)).astype(
        jnp.bfloat16
    )
    return (feature_adjoint, triple_projector_adjoint, emitted_adjoint)


HALVING_BITS = ((3, 1, 4, 2, 5, 6), (1, 4, 3, 5, 6, 2))


def tree_all_reduce(parts):
    devices = lax.axis_size("grp") * lax.axis_size("seq")
    flat = jnp.concatenate([part.reshape(-1) for part in parts])
    rows = -(-flat.size // (devices * 128 * 8)) * 8
    flat = jnp.pad(flat, (0, devices * rows * 128 - flat.size))
    block = flat.reshape(devices, rows, 128)
    me = lax.axis_index("grp") * lax.axis_size("seq") + lax.axis_index("seq")
    core = me & 1
    steps = [(0, 0)] + list(zip(*HALVING_BITS))

    def mask_of(step):
        return lambda j: step[j & 1]

    def bit_of(step):
        return jnp.where(core == 0, step[0], step[1])

    for step in steps:
        pick = mask_of(step)
        perm = [(j, j ^ (1 << pick(j))) for j in range(devices)]
        half = block.shape[0] // 2
        side = (me >> bit_of(step)) & 1
        keep = lax.dynamic_slice_in_dim(block, side * half, half, 0)
        send = lax.dynamic_slice_in_dim(block, (1 - side) * half, half, 0)
        got = lax.ppermute(send.astype(jnp.bfloat16), ("grp", "seq"), perm)
        block = keep + got.astype(jnp.float32)
    block = block.astype(jnp.bfloat16)
    for step in reversed(steps):
        pick = mask_of(step)
        perm = [(j, j ^ (1 << pick(j))) for j in range(devices)]
        side = (me >> bit_of(step)) & 1
        got = lax.ppermute(block, ("grp", "seq"), perm)
        size = block.shape[0]
        whole = jnp.zeros((2 * size,) + block.shape[1:], block.dtype)
        whole = lax.dynamic_update_slice_in_dim(whole, block, side * size, 0)
        block = lax.dynamic_update_slice_in_dim(whole, got, (1 - side) * size, 0)
    flat = block.reshape(-1).astype(jnp.float32)
    sums = []
    start = 0
    for part in parts:
        sums.append(flat[start : start + part.size].reshape(part.shape))
        start += part.size
    return tuple(sums)


def body(
    clip_latents, adjoint_seed, kernel_matrix, triple_projector, exit_projector, logit_scaling
):
    frames = clip_latents.shape[1]
    height = clip_latents.shape[2]
    channels = exit_projector.shape[0]
    breadth = clip_latents.shape[3] // channels
    places = height * breadth
    source = clip_latents.reshape(frames, height, breadth, channels)
    latent_features, patches, pull_act = spatial_forward(source, kernel_matrix)
    placed_features = lax.all_to_all(
        latent_features.reshape(frames, places, channels),
        "seq",
        split_axis=1,
        concat_axis=0,
        tiled=True,
    )
    section_outcome, standardised_tokens, mapped_tokens, softmax_blend = temporal_mixing_apply(
        placed_features, triple_projector, exit_projector, logit_scaling
    )
    output = lax.all_to_all(
        section_outcome, "seq", split_axis=0, concat_axis=1, tiled=True
    ).reshape(clip_latents.shape)
    upstream_adjoint = lax.all_to_all(
        adjoint_seed.reshape(frames, places, channels),
        "seq",
        split_axis=1,
        concat_axis=0,
        tiled=True,
    )
    feature_adjoint, triple_projector_adjoint, emitted_adjoint = temporal_mixing_reverse(
        placed_features,
        upstream_adjoint,
        standardised_tokens,
        mapped_tokens,
        softmax_blend,
        triple_projector,
        exit_projector,
        logit_scaling,
    )
    back_frames = lax.all_to_all(feature_adjoint, "seq", split_axis=0, concat_axis=1, tiled=True)
    d_source, grad_conv = spatial_backward(
        back_frames.reshape(frames * places, channels),
        patches,
        pull_act,
        kernel_matrix,
        frames,
        height,
        breadth,
    )
    d_video = d_source.reshape(clip_latents.shape)
    sum_conv, sum_qkv, sum_out = tree_all_reduce(
        (grad_conv, triple_projector_adjoint, emitted_adjoint)
    )
    factor = 1.0 / math.sqrt(lax.axis_size("grp") * lax.axis_size("seq") * frames * places)
    return (output, d_video, sum_conv * factor, sum_qkv * factor, sum_out * factor)


def solution(mesh):
    return jax.shard_map(
        body,
        mesh=mesh,
        in_specs=(P("grp", "seq", None, None), P("grp", "seq", None, None), P(), P(), P(), P()),
        out_specs=(P("grp", "seq", None, None), P("grp", "seq", None, None), P(), P(), P()),
        check_vma=False,
    )
```

```python
import math

import jax
import jax.numpy as jnp
from jax import lax
from jax.sharding import PartitionSpec as P

HEAD_DIM = 64
GROUPS = 32


def group_act(widened):
    frames, height, breadth, channels = widened.shape
    span = channels // GROUPS
    count = height * breadth * span
    tokens = widened.reshape(frames, height * breadth, channels)

    def per_group(column_sums):
        totals = column_sums.reshape(frames, GROUPS, span).sum(axis=-1) / count
        return jnp.repeat(totals, span, axis=-1)[:, None, :]

    centre = per_group(jnp.sum(tokens, axis=1))
    shifted = tokens - centre
    spread = per_group(jnp.sum(jnp.square(shifted), axis=1))
    normed = shifted * lax.rsqrt(spread + 1e-05)
    return jax.nn.silu(normed).reshape(frames, height, breadth, channels)


def make_patches(active):
    frames, height, breadth, channels = active.shape
    padded = jnp.pad(active, ((0, 0), (1, 1), (1, 1), (0, 0)))
    pieces = [
        padded[:, down_step : down_step + height, side_step : side_step + breadth, :]
        for down_step in range(3)
        for side_step in range(3)
    ]
    return jnp.concatenate(pieces, axis=-1).reshape(frames * height * breadth, 9 * channels)


def fold_patches(columns, frames, height, breadth):
    channels = columns.shape[-1] // 9
    pieces = columns.reshape(frames, height, breadth, 9, channels)
    totals = jnp.zeros((frames, height + 2, breadth + 2, channels), jnp.float32)
    for down_step in range(3):
        for side_step in range(3):
            shifted = pieces[:, :, :, down_step * 3 + side_step, :]
            totals = totals + jnp.pad(
                shifted, ((0, 0), (down_step, 2 - down_step), (side_step, 2 - side_step), (0, 0))
            )
    return totals[:, 1 : height + 1, 1 : breadth + 1, :]


def layer_norm(widened):
    centre = jnp.mean(widened, axis=-1, keepdims=True)
    spread = jnp.mean(jnp.square(widened - centre), axis=-1, keepdims=True)
    return (widened - centre) * lax.rsqrt(spread + 1e-05)


def head_mixing(query, keys, values, scaling):
    query = (
        query * lax.rsqrt(jnp.sum(query * query, axis=-1, keepdims=True) + 1e-06) * scaling
    ).astype(jnp.bfloat16)
    keys = (keys * lax.rsqrt(jnp.sum(keys * keys, axis=-1, keepdims=True) + 1e-06)).astype(
        jnp.bfloat16
    )
    values = values.astype(jnp.bfloat16)
    scores = jnp.einsum("fld,gld->lfg", query, keys, preferred_element_type=jnp.float32)
    weights = jnp.exp(scores)
    weights = (weights / jnp.sum(weights, axis=-1, keepdims=True)).astype(jnp.bfloat16)
    return jnp.einsum("lfg,gld->fld", weights, values, preferred_element_type=jnp.float32)


def temporal_mixing(mapped_tokens, logit_scaling):
    frames, places, triple = mapped_tokens.shape
    channels = triple // 3
    head_count = channels // HEAD_DIM
    blends = []
    for head in range(head_count):
        low = head * HEAD_DIM
        blends.append(
            head_mixing(
                mapped_tokens[:, :, low : low + HEAD_DIM],
                mapped_tokens[:, :, channels + low : channels + low + HEAD_DIM],
                mapped_tokens[:, :, 2 * channels + low : 2 * channels + low + HEAD_DIM],
                logit_scaling[head],
            )
        )
    return jnp.concatenate(blends, axis=-1)


def contract_rows(left, right):
    return lax.dot_general(
        left, right, (((0,), (0,)), ((), ())), preferred_element_type=jnp.float32
    )


def spatial_forward(source, kernel_matrix):
    frames, height, breadth, channels = source.shape
    widened = source.astype(jnp.float32)
    active, pull_act = jax.vjp(group_act, widened)
    patches = make_patches(active.astype(jnp.bfloat16))
    convolved = jnp.dot(patches, kernel_matrix, preferred_element_type=jnp.float32)
    latent_features = (widened.reshape(frames * height * breadth, channels) + convolved).astype(
        jnp.bfloat16
    )
    return (latent_features, patches, pull_act)


def spatial_backward(upstream_adjoint, patches, pull_act, kernel_matrix, frames, height, breadth):
    channels = upstream_adjoint.shape[-1]
    grad_conv = contract_rows(patches, upstream_adjoint)
    columns = jnp.dot(upstream_adjoint, kernel_matrix.T, preferred_element_type=jnp.float32)
    d_active = fold_patches(columns, frames, height, breadth)
    d_source = pull_act(d_active)[0]
    section_outcome = (
        upstream_adjoint.astype(jnp.float32).reshape(frames, height, breadth, channels) + d_source
    ).astype(jnp.bfloat16)
    return (section_outcome, grad_conv)


def temporal_mixing_apply(latent_features, triple_projector, exit_projector, logit_scaling):
    frames, places, channels = latent_features.shape
    widened = latent_features.astype(jnp.float32)
    standardised_tokens = layer_norm(widened).astype(jnp.bfloat16)
    mapped_tokens = jnp.dot(
        standardised_tokens.reshape(frames * places, channels),
        triple_projector,
        preferred_element_type=jnp.float32,
    ).reshape(frames, places, 3 * channels)
    softmax_blend = temporal_mixing(mapped_tokens, logit_scaling).astype(jnp.bfloat16)
    branch = jnp.dot(
        softmax_blend.reshape(frames * places, channels),
        exit_projector,
        preferred_element_type=jnp.float32,
    )
    section_outcome = (widened + branch.reshape(frames, places, channels)).astype(jnp.bfloat16)
    return (section_outcome, standardised_tokens, mapped_tokens, softmax_blend)


def temporal_mixing_reverse(
    latent_features,
    upstream_adjoint,
    standardised_tokens,
    mapped_tokens,
    softmax_blend,
    triple_projector,
    exit_projector,
    logit_scaling,
):
    frames, places, channels = latent_features.shape
    rows_cot = upstream_adjoint.reshape(frames * places, channels)
    emitted_adjoint = contract_rows(softmax_blend.reshape(frames * places, channels), rows_cot)
    d_mixture = jnp.dot(rows_cot, exit_projector.T, preferred_element_type=jnp.float32).astype(
        jnp.bfloat16
    )
    discarded_item, temporal_mixing_adjoint = jax.vjp(
        lambda entry_tensor: temporal_mixing(entry_tensor, logit_scaling), mapped_tokens
    )
    d_projected = temporal_mixing_adjoint(
        d_mixture.astype(jnp.float32).reshape(frames, places, channels)
    )[0].astype(jnp.bfloat16)
    rows_proj = d_projected.reshape(frames * places, 3 * channels)
    triple_projector_adjoint = contract_rows(
        standardised_tokens.reshape(frames * places, channels), rows_proj
    )
    d_normed = jnp.dot(rows_proj, triple_projector.T, preferred_element_type=jnp.float32).reshape(
        frames, places, channels
    )
    discarded_item, pull_norm = jax.vjp(layer_norm, latent_features.astype(jnp.float32))
    d_layer = pull_norm(d_normed)[0].astype(jnp.bfloat16)
    feature_adjoint = (upstream_adjoint.astype(jnp.float32) + d_layer.astype(jnp.float32)).astype(
        jnp.bfloat16
    )
    return (feature_adjoint, triple_projector_adjoint, emitted_adjoint)


HALVING_BITS = ((3, 1, 4, 2, 5, 6), (1, 4, 3, 5, 6, 2))


def tree_all_reduce(parts):
    devices = lax.axis_size("grp") * lax.axis_size("seq")
    flat = jnp.concatenate([part.reshape(-1) for part in parts])
    rows = -(-flat.size // (devices * 128 * 8)) * 8
    flat = jnp.pad(flat, (0, devices * rows * 128 - flat.size))
    block = flat.reshape(devices, rows, 128)
    me = lax.axis_index("grp") * lax.axis_size("seq") + lax.axis_index("seq")
    core = me & 1
    steps = [(0, 0)] + list(zip(*HALVING_BITS))

    def mask_of(step):
        return lambda j: step[j & 1]

    def bit_of(step):
        return jnp.where(core == 0, step[0], step[1])

    for step in steps:
        pick = mask_of(step)
        perm = [(j, j ^ (1 << pick(j))) for j in range(devices)]
        half = block.shape[0] // 2
        side = (me >> bit_of(step)) & 1
        keep = lax.dynamic_slice_in_dim(block, side * half, half, 0)
        send = lax.dynamic_slice_in_dim(block, (1 - side) * half, half, 0)
        got = lax.ppermute(send.astype(jnp.bfloat16), ("grp", "seq"), perm)
        block = keep + got.astype(jnp.float32)
    block = block.astype(jnp.bfloat16)
    for step in reversed(steps):
        pick = mask_of(step)
        perm = [(j, j ^ (1 << pick(j))) for j in range(devices)]
        side = (me >> bit_of(step)) & 1
        got = lax.ppermute(block, ("grp", "seq"), perm)
        size = block.shape[0]
        whole = jnp.zeros((2 * size,) + block.shape[1:], block.dtype)
        whole = lax.dynamic_update_slice_in_dim(whole, block, side * size, 0)
        block = lax.dynamic_update_slice_in_dim(whole, got, (1 - side) * size, 0)
    flat = block.reshape(-1).astype(jnp.float32)
    sums = []
    start = 0
    for part in parts:
        sums.append(flat[start : start + part.size].reshape(part.shape))
        start += part.size
    return tuple(sums)


def body(
    clip_latents, adjoint_seed, kernel_matrix, triple_projector, exit_projector, logit_scaling
):
    frames = clip_latents.shape[1]
    height = clip_latents.shape[2]
    channels = exit_projector.shape[0]
    breadth = clip_latents.shape[3] // channels
    places = height * breadth
    source = clip_latents.reshape(frames, height, breadth, channels)
    latent_features, patches, pull_act = spatial_forward(source, kernel_matrix)
    placed_features = lax.all_to_all(
        latent_features.reshape(frames, places, channels),
        "seq",
        split_axis=1,
        concat_axis=0,
        tiled=True,
    )
    section_outcome, standardised_tokens, mapped_tokens, softmax_blend = temporal_mixing_apply(
        placed_features, triple_projector, exit_projector, logit_scaling
    )
    output = lax.all_to_all(
        section_outcome, "seq", split_axis=0, concat_axis=1, tiled=True
    ).reshape(clip_latents.shape)
    upstream_adjoint = lax.all_to_all(
        adjoint_seed.reshape(frames, places, channels),
        "seq",
        split_axis=1,
        concat_axis=0,
        tiled=True,
    )
    feature_adjoint, triple_projector_adjoint, emitted_adjoint = temporal_mixing_reverse(
        placed_features,
        upstream_adjoint,
        standardised_tokens,
        mapped_tokens,
        softmax_blend,
        triple_projector,
        exit_projector,
        logit_scaling,
    )
    back_frames = lax.all_to_all(feature_adjoint, "seq", split_axis=0, concat_axis=1, tiled=True)
    d_source, grad_conv = spatial_backward(
        back_frames.reshape(frames * places, channels),
        patches,
        pull_act,
        kernel_matrix,
        frames,
        height,
        breadth,
    )
    d_video = d_source.reshape(clip_latents.shape)
    sum_conv, sum_qkv, sum_out = tree_all_reduce(
        (grad_conv, triple_projector_adjoint, emitted_adjoint)
    )
    factor = 1.0 / math.sqrt(lax.axis_size("grp") * lax.axis_size("seq") * frames * places)
    return (output, d_video, sum_conv * factor, sum_qkv * factor, sum_out * factor)


def solution(mesh):
    return jax.shard_map(
        body,
        mesh=mesh,
        in_specs=(P("grp", "seq", None, None), P("grp", "seq", None, None), P(), P(), P(), P()),
        out_specs=(P("grp", "seq", None, None), P("grp", "seq", None, None), P(), P(), P()),
        check_vma=False,
    )
```

```python
import math

import jax
import jax.numpy as jnp
from jax import lax
from jax.sharding import PartitionSpec as P

HEAD_DIM = 64
GROUPS = 32


def group_act(widened):
    frames, height, breadth, channels = widened.shape
    span = channels // GROUPS
    count = height * breadth * span
    tokens = widened.reshape(frames, height * breadth, channels)

    def per_group(column_sums):
        totals = column_sums.reshape(frames, GROUPS, span).sum(axis=-1) / count
        return jnp.repeat(totals, span, axis=-1)[:, None, :]

    centre = per_group(jnp.sum(tokens, axis=1))
    shifted = tokens - centre
    spread = per_group(jnp.sum(jnp.square(shifted), axis=1))
    normed = shifted * lax.rsqrt(spread + 1e-05)
    return jax.nn.silu(normed).reshape(frames, height, breadth, channels)


def make_patches(active):
    frames, height, breadth, channels = active.shape
    padded = jnp.pad(active, ((0, 0), (1, 1), (1, 1), (0, 0)))
    pieces = [
        padded[:, down_step : down_step + height, side_step : side_step + breadth, :]
        for down_step in range(3)
        for side_step in range(3)
    ]
    return jnp.concatenate(pieces, axis=-1).reshape(frames * height * breadth, 9 * channels)


def fold_patches(columns, frames, height, breadth):
    channels = columns.shape[-1] // 9
    pieces = columns.reshape(frames, height, breadth, 9, channels)
    totals = jnp.zeros((frames, height + 2, breadth + 2, channels), jnp.float32)
    for down_step in range(3):
        for side_step in range(3):
            shifted = pieces[:, :, :, down_step * 3 + side_step, :]
            totals = totals + jnp.pad(
                shifted, ((0, 0), (down_step, 2 - down_step), (side_step, 2 - side_step), (0, 0))
            )
    return totals[:, 1 : height + 1, 1 : breadth + 1, :]


def layer_norm(widened):
    centre = jnp.mean(widened, axis=-1, keepdims=True)
    spread = jnp.mean(jnp.square(widened - centre), axis=-1, keepdims=True)
    return (widened - centre) * lax.rsqrt(spread + 1e-05)


def head_mixing(query, keys, values, scaling):
    query = (
        query * lax.rsqrt(jnp.sum(query * query, axis=-1, keepdims=True) + 1e-06) * scaling
    ).astype(jnp.bfloat16)
    keys = (keys * lax.rsqrt(jnp.sum(keys * keys, axis=-1, keepdims=True) + 1e-06)).astype(
        jnp.bfloat16
    )
    values = values.astype(jnp.bfloat16)
    scores = jnp.einsum("fld,gld->lfg", query, keys, preferred_element_type=jnp.float32)
    weights = jnp.exp(scores)
    weights = (weights / jnp.sum(weights, axis=-1, keepdims=True)).astype(jnp.bfloat16)
    return jnp.einsum("lfg,gld->fld", weights, values, preferred_element_type=jnp.float32)


def temporal_mixing(mapped_tokens, logit_scaling):
    frames, places, triple = mapped_tokens.shape
    channels = triple // 3
    head_count = channels // HEAD_DIM
    blends = []
    for head in range(head_count):
        low = head * HEAD_DIM
        blends.append(
            head_mixing(
                mapped_tokens[:, :, low : low + HEAD_DIM],
                mapped_tokens[:, :, channels + low : channels + low + HEAD_DIM],
                mapped_tokens[:, :, 2 * channels + low : 2 * channels + low + HEAD_DIM],
                logit_scaling[head],
            )
        )
    return jnp.concatenate(blends, axis=-1)


def contract_rows(left, right):
    return lax.dot_general(
        left, right, (((0,), (0,)), ((), ())), preferred_element_type=jnp.float32
    )


def spatial_forward(source, kernel_matrix):
    frames, height, breadth, channels = source.shape
    widened = source.astype(jnp.float32)
    active, pull_act = jax.vjp(group_act, widened)
    patches = make_patches(active.astype(jnp.bfloat16))
    convolved = jnp.dot(patches, kernel_matrix, preferred_element_type=jnp.float32)
    latent_features = (widened.reshape(frames * height * breadth, channels) + convolved).astype(
        jnp.bfloat16
    )
    return (latent_features, patches, pull_act)


def spatial_backward(upstream_adjoint, patches, pull_act, kernel_matrix, frames, height, breadth):
    channels = upstream_adjoint.shape[-1]
    grad_conv = contract_rows(patches, upstream_adjoint)
    columns = jnp.dot(upstream_adjoint, kernel_matrix.T, preferred_element_type=jnp.float32)
    d_active = fold_patches(columns, frames, height, breadth)
    d_source = pull_act(d_active)[0]
    section_outcome = (
        upstream_adjoint.astype(jnp.float32).reshape(frames, height, breadth, channels) + d_source
    ).astype(jnp.bfloat16)
    return (section_outcome, grad_conv)


def temporal_mixing_apply(latent_features, triple_projector, exit_projector, logit_scaling):
    frames, places, channels = latent_features.shape
    widened = latent_features.astype(jnp.float32)
    standardised_tokens = layer_norm(widened).astype(jnp.bfloat16)
    mapped_tokens = jnp.dot(
        standardised_tokens.reshape(frames * places, channels),
        triple_projector,
        preferred_element_type=jnp.float32,
    ).reshape(frames, places, 3 * channels)
    softmax_blend = temporal_mixing(mapped_tokens, logit_scaling).astype(jnp.bfloat16)
    branch = jnp.dot(
        softmax_blend.reshape(frames * places, channels),
        exit_projector,
        preferred_element_type=jnp.float32,
    )
    section_outcome = (widened + branch.reshape(frames, places, channels)).astype(jnp.bfloat16)
    return (section_outcome, standardised_tokens, mapped_tokens, softmax_blend)


def temporal_mixing_reverse(
    latent_features,
    upstream_adjoint,
    standardised_tokens,
    mapped_tokens,
    softmax_blend,
    triple_projector,
    exit_projector,
    logit_scaling,
):
    frames, places, channels = latent_features.shape
    rows_cot = upstream_adjoint.reshape(frames * places, channels)
    emitted_adjoint = contract_rows(softmax_blend.reshape(frames * places, channels), rows_cot)
    d_mixture = jnp.dot(rows_cot, exit_projector.T, preferred_element_type=jnp.float32).astype(
        jnp.bfloat16
    )
    discarded_item, temporal_mixing_adjoint = jax.vjp(
        lambda entry_tensor: temporal_mixing(entry_tensor, logit_scaling), mapped_tokens
    )
    d_projected = temporal_mixing_adjoint(
        d_mixture.astype(jnp.float32).reshape(frames, places, channels)
    )[0].astype(jnp.bfloat16)
    rows_proj = d_projected.reshape(frames * places, 3 * channels)
    triple_projector_adjoint = contract_rows(
        standardised_tokens.reshape(frames * places, channels), rows_proj
    )
    d_normed = jnp.dot(rows_proj, triple_projector.T, preferred_element_type=jnp.float32).reshape(
        frames, places, channels
    )
    discarded_item, pull_norm = jax.vjp(layer_norm, latent_features.astype(jnp.float32))
    d_layer = pull_norm(d_normed)[0].astype(jnp.bfloat16)
    feature_adjoint = (upstream_adjoint.astype(jnp.float32) + d_layer.astype(jnp.float32)).astype(
        jnp.bfloat16
    )
    return (feature_adjoint, triple_projector_adjoint, emitted_adjoint)


CORE_BITS = (0,)
AXIS_BITS = {"x": (3, 6), "y": (4, 5), "z": (1, 2)}
ROUNDS = (("x", "z", "y"), ("z", "y", "x"))


def tree_all_reduce(parts):
    devices = lax.axis_size("grp") * lax.axis_size("seq")
    flat = jnp.concatenate([part.reshape(-1) for part in parts])
    rows = -(-flat.size // (devices * 128 * 8)) * 8
    flat = jnp.pad(flat, (0, devices * rows * 128 - flat.size))
    block = flat.reshape(devices, rows, 128)
    me = lax.axis_index("grp") * lax.axis_size("seq") + lax.axis_index("seq")
    core = me & 1
    rounds = [(CORE_BITS, CORE_BITS)] + [
        (AXIS_BITS[first], AXIS_BITS[second]) for first, second in zip(*ROUNDS)
    ]

    def flip(j, bits, mask):
        for place, bit in enumerate(bits):
            if (mask >> place) & 1:
                j ^= 1 << bit
        return j

    def position(bits):
        return sum(((me >> bit) & 1) << place for place, bit in enumerate(bits))

    def plan(choice):
        size = 1 << len(choice[0])
        spot = jnp.where(core == 0, position(choice[0]), position(choice[1]))
        perms = [
            [(j, flip(j, choice[j & 1], mask)) for j in range(devices)] for mask in range(1, size)
        ]
        return size, spot, perms

    for choice in rounds:
        size, spot, perms = plan(choice)
        piece = block.shape[0] // size
        total = lax.dynamic_slice_in_dim(block, spot * piece, piece, 0)
        for mask, perm in zip(range(1, size), perms):
            send = lax.dynamic_slice_in_dim(block, (spot ^ mask) * piece, piece, 0)
            got = lax.ppermute(send.astype(jnp.bfloat16), ("grp", "seq"), perm)
            total = total + got.astype(jnp.float32)
        block = total
    block = block.astype(jnp.bfloat16)
    for choice in reversed(rounds):
        size, spot, perms = plan(choice)
        piece = block.shape[0]
        whole = jnp.zeros((size * piece,) + block.shape[1:], block.dtype)
        whole = lax.dynamic_update_slice_in_dim(whole, block, spot * piece, 0)
        for mask, perm in zip(range(1, size), perms):
            got = lax.ppermute(block, ("grp", "seq"), perm)
            whole = lax.dynamic_update_slice_in_dim(whole, got, (spot ^ mask) * piece, 0)
        block = whole
    flat = block.reshape(-1).astype(jnp.float32)
    sums = []
    start = 0
    for part in parts:
        sums.append(flat[start : start + part.size].reshape(part.shape))
        start += part.size
    return tuple(sums)


def body(
    clip_latents, adjoint_seed, kernel_matrix, triple_projector, exit_projector, logit_scaling
):
    frames = clip_latents.shape[1]
    height = clip_latents.shape[2]
    channels = exit_projector.shape[0]
    breadth = clip_latents.shape[3] // channels
    places = height * breadth
    source = clip_latents.reshape(frames, height, breadth, channels)
    latent_features, patches, pull_act = spatial_forward(source, kernel_matrix)
    placed_features = lax.all_to_all(
        latent_features.reshape(frames, places, channels),
        "seq",
        split_axis=1,
        concat_axis=0,
        tiled=True,
    )
    section_outcome, standardised_tokens, mapped_tokens, softmax_blend = temporal_mixing_apply(
        placed_features, triple_projector, exit_projector, logit_scaling
    )
    output = lax.all_to_all(
        section_outcome, "seq", split_axis=0, concat_axis=1, tiled=True
    ).reshape(clip_latents.shape)
    upstream_adjoint = lax.all_to_all(
        adjoint_seed.reshape(frames, places, channels),
        "seq",
        split_axis=1,
        concat_axis=0,
        tiled=True,
    )
    feature_adjoint, triple_projector_adjoint, emitted_adjoint = temporal_mixing_reverse(
        placed_features,
        upstream_adjoint,
        standardised_tokens,
        mapped_tokens,
        softmax_blend,
        triple_projector,
        exit_projector,
        logit_scaling,
    )
    back_frames = lax.all_to_all(feature_adjoint, "seq", split_axis=0, concat_axis=1, tiled=True)
    d_source, grad_conv = spatial_backward(
        back_frames.reshape(frames * places, channels),
        patches,
        pull_act,
        kernel_matrix,
        frames,
        height,
        breadth,
    )
    d_video = d_source.reshape(clip_latents.shape)
    sum_conv, sum_qkv, sum_out = tree_all_reduce(
        (grad_conv, triple_projector_adjoint, emitted_adjoint)
    )
    factor = 1.0 / math.sqrt(lax.axis_size("grp") * lax.axis_size("seq") * frames * places)
    return (output, d_video, sum_conv * factor, sum_qkv * factor, sum_out * factor)


def solution(mesh):
    return jax.shard_map(
        body,
        mesh=mesh,
        in_specs=(P("grp", "seq", None, None), P("grp", "seq", None, None), P(), P(), P(), P()),
        out_specs=(P("grp", "seq", None, None), P("grp", "seq", None, None), P(), P(), P()),
        check_vma=False,
    )
```

```python
import math

import jax
import jax.numpy as jnp
from jax import lax
from jax.sharding import PartitionSpec as P

HEAD_DIM = 64
GROUPS = 32


def group_act(widened):
    frames, height, breadth, channels = widened.shape
    span = channels // GROUPS
    count = height * breadth * span
    tokens = widened.reshape(frames, height * breadth, channels)

    def per_group(column_sums):
        totals = column_sums.reshape(frames, GROUPS, span).sum(axis=-1) / count
        return jnp.repeat(totals, span, axis=-1)[:, None, :]

    centre = per_group(jnp.sum(tokens, axis=1))
    shifted = tokens - centre
    spread = per_group(jnp.sum(jnp.square(shifted), axis=1))
    normed = shifted * lax.rsqrt(spread + 1e-05)
    return jax.nn.silu(normed).reshape(frames, height, breadth, channels)


def make_patches(active):
    frames, height, breadth, channels = active.shape
    padded = jnp.pad(active, ((0, 0), (1, 1), (1, 1), (0, 0)))
    pieces = [
        padded[:, down_step : down_step + height, side_step : side_step + breadth, :]
        for down_step in range(3)
        for side_step in range(3)
    ]
    return jnp.concatenate(pieces, axis=-1).reshape(frames * height * breadth, 9 * channels)


def fold_patches(columns, frames, height, breadth):
    channels = columns.shape[-1] // 9
    pieces = columns.reshape(frames, height, breadth, 9, channels)
    totals = jnp.zeros((frames, height + 2, breadth + 2, channels), jnp.float32)
    for down_step in range(3):
        for side_step in range(3):
            shifted = pieces[:, :, :, down_step * 3 + side_step, :]
            totals = totals + jnp.pad(
                shifted, ((0, 0), (down_step, 2 - down_step), (side_step, 2 - side_step), (0, 0))
            )
    return totals[:, 1 : height + 1, 1 : breadth + 1, :]


def layer_norm(widened):
    centre = jnp.mean(widened, axis=-1, keepdims=True)
    spread = jnp.mean(jnp.square(widened - centre), axis=-1, keepdims=True)
    return (widened - centre) * lax.rsqrt(spread + 1e-05)


def temporal_mixing(mapped_tokens, logit_scaling):
    frames, places, triple = mapped_tokens.shape
    channels = triple // 3
    head_count = channels // HEAD_DIM
    pieces = mapped_tokens.reshape(frames, places, 3, head_count, HEAD_DIM)
    query = pieces[:, :, 0]
    keys = pieces[:, :, 1]
    values = pieces[:, :, 2].astype(jnp.bfloat16)
    query = (
        query
        * lax.rsqrt(jnp.sum(query * query, axis=-1, keepdims=True) + 1e-06)
        * logit_scaling[:, None]
    ).astype(jnp.bfloat16)
    keys = (keys * lax.rsqrt(jnp.sum(keys * keys, axis=-1, keepdims=True) + 1e-06)).astype(
        jnp.bfloat16
    )
    scores = jnp.einsum("flhd,glhd->lhfg", query, keys, preferred_element_type=jnp.float32)
    weights = jnp.exp(scores)
    weights = (weights / jnp.sum(weights, axis=-1, keepdims=True)).astype(jnp.bfloat16)
    blend = jnp.einsum("lhfg,glhd->flhd", weights, values, preferred_element_type=jnp.float32)
    return blend.reshape(frames, places, channels)


def contract_rows(left, right):
    return lax.dot_general(
        left, right, (((0,), (0,)), ((), ())), preferred_element_type=jnp.float32
    )


def spatial_forward(source, kernel_matrix):
    frames, height, breadth, channels = source.shape
    widened = source.astype(jnp.float32)
    active, pull_act = jax.vjp(group_act, widened)
    patches = make_patches(active.astype(jnp.bfloat16))
    convolved = jnp.dot(patches, kernel_matrix, preferred_element_type=jnp.float32)
    latent_features = (widened.reshape(frames * height * breadth, channels) + convolved).astype(
        jnp.bfloat16
    )
    return (latent_features, patches, pull_act)


def spatial_backward(upstream_adjoint, patches, pull_act, kernel_matrix, frames, height, breadth):
    channels = upstream_adjoint.shape[-1]
    grad_conv = contract_rows(patches, upstream_adjoint)
    columns = jnp.dot(upstream_adjoint, kernel_matrix.T, preferred_element_type=jnp.float32)
    d_active = fold_patches(columns, frames, height, breadth)
    d_source = pull_act(d_active)[0]
    section_outcome = (
        upstream_adjoint.astype(jnp.float32).reshape(frames, height, breadth, channels) + d_source
    ).astype(jnp.bfloat16)
    return (section_outcome, grad_conv)


def temporal_mixing_apply(latent_features, triple_projector, exit_projector, logit_scaling):
    frames, places, channels = latent_features.shape
    widened = latent_features.astype(jnp.float32)
    standardised_tokens = layer_norm(widened).astype(jnp.bfloat16)
    mapped_tokens = jnp.dot(
        standardised_tokens.reshape(frames * places, channels),
        triple_projector,
        preferred_element_type=jnp.float32,
    ).reshape(frames, places, 3 * channels)
    softmax_blend = temporal_mixing(mapped_tokens, logit_scaling).astype(jnp.bfloat16)
    branch = jnp.dot(
        softmax_blend.reshape(frames * places, channels),
        exit_projector,
        preferred_element_type=jnp.float32,
    )
    section_outcome = (widened + branch.reshape(frames, places, channels)).astype(jnp.bfloat16)
    return (section_outcome, standardised_tokens, mapped_tokens, softmax_blend)


def temporal_mixing_reverse(
    latent_features,
    upstream_adjoint,
    standardised_tokens,
    mapped_tokens,
    softmax_blend,
    triple_projector,
    exit_projector,
    logit_scaling,
):
    frames, places, channels = latent_features.shape
    rows_cot = upstream_adjoint.reshape(frames * places, channels)
    emitted_adjoint = contract_rows(softmax_blend.reshape(frames * places, channels), rows_cot)
    d_mixture = jnp.dot(rows_cot, exit_projector.T, preferred_element_type=jnp.float32).astype(
        jnp.bfloat16
    )
    discarded_item, temporal_mixing_adjoint = jax.vjp(
        lambda entry_tensor: temporal_mixing(entry_tensor, logit_scaling), mapped_tokens
    )
    d_projected = temporal_mixing_adjoint(
        d_mixture.astype(jnp.float32).reshape(frames, places, channels)
    )[0].astype(jnp.bfloat16)
    rows_proj = d_projected.reshape(frames * places, 3 * channels)
    triple_projector_adjoint = contract_rows(
        standardised_tokens.reshape(frames * places, channels), rows_proj
    )
    d_normed = jnp.dot(rows_proj, triple_projector.T, preferred_element_type=jnp.float32).reshape(
        frames, places, channels
    )
    discarded_item, pull_norm = jax.vjp(layer_norm, latent_features.astype(jnp.float32))
    d_layer = pull_norm(d_normed)[0].astype(jnp.bfloat16)
    feature_adjoint = (upstream_adjoint.astype(jnp.float32) + d_layer.astype(jnp.float32)).astype(
        jnp.bfloat16
    )
    return (feature_adjoint, triple_projector_adjoint, emitted_adjoint)


CORE_BITS = (0,)
AXIS_BITS = {"x": (3, 6), "y": (4, 5), "z": (1, 2)}
ROUNDS = (("x", "z", "y"), ("z", "y", "x"))


def tree_all_reduce(parts):
    devices = lax.axis_size("grp") * lax.axis_size("seq")
    flat = jnp.concatenate([part.reshape(-1) for part in parts])
    rows = -(-flat.size // (devices * 128 * 8)) * 8
    flat = jnp.pad(flat, (0, devices * rows * 128 - flat.size))
    block = flat.reshape(devices, rows, 128)
    me = lax.axis_index("grp") * lax.axis_size("seq") + lax.axis_index("seq")
    core = me & 1
    rounds = [(CORE_BITS, CORE_BITS)] + [
        (AXIS_BITS[first], AXIS_BITS[second]) for first, second in zip(*ROUNDS)
    ]

    def flip(j, bits, mask):
        for place, bit in enumerate(bits):
            if (mask >> place) & 1:
                j ^= 1 << bit
        return j

    def position(bits):
        return sum(((me >> bit) & 1) << place for place, bit in enumerate(bits))

    def plan(choice):
        size = 1 << len(choice[0])
        spot = jnp.where(core == 0, position(choice[0]), position(choice[1]))
        perms = [
            [(j, flip(j, choice[j & 1], mask)) for j in range(devices)] for mask in range(1, size)
        ]
        return size, spot, perms

    for choice in rounds:
        size, spot, perms = plan(choice)
        piece = block.shape[0] // size
        total = lax.dynamic_slice_in_dim(block, spot * piece, piece, 0)
        for mask, perm in zip(range(1, size), perms):
            send = lax.dynamic_slice_in_dim(block, (spot ^ mask) * piece, piece, 0)
            got = lax.ppermute(send.astype(jnp.bfloat16), ("grp", "seq"), perm)
            total = total + got.astype(jnp.float32)
        block = total
    block = block.astype(jnp.bfloat16)
    for choice in reversed(rounds):
        size, spot, perms = plan(choice)
        piece = block.shape[0]
        whole = jnp.zeros((size * piece,) + block.shape[1:], block.dtype)
        whole = lax.dynamic_update_slice_in_dim(whole, block, spot * piece, 0)
        for mask, perm in zip(range(1, size), perms):
            got = lax.ppermute(block, ("grp", "seq"), perm)
            whole = lax.dynamic_update_slice_in_dim(whole, got, (spot ^ mask) * piece, 0)
        block = whole
    flat = block.reshape(-1).astype(jnp.float32)
    sums = []
    start = 0
    for part in parts:
        sums.append(flat[start : start + part.size].reshape(part.shape))
        start += part.size
    return tuple(sums)


def body(
    clip_latents, adjoint_seed, kernel_matrix, triple_projector, exit_projector, logit_scaling
):
    frames = clip_latents.shape[1]
    height = clip_latents.shape[2]
    channels = exit_projector.shape[0]
    breadth = clip_latents.shape[3] // channels
    places = height * breadth
    source = clip_latents.reshape(frames, height, breadth, channels)
    latent_features, patches, pull_act = spatial_forward(source, kernel_matrix)
    placed_features = lax.all_to_all(
        latent_features.reshape(frames, places, channels),
        "seq",
        split_axis=1,
        concat_axis=0,
        tiled=True,
    )
    section_outcome, standardised_tokens, mapped_tokens, softmax_blend = temporal_mixing_apply(
        placed_features, triple_projector, exit_projector, logit_scaling
    )
    output = lax.all_to_all(
        section_outcome, "seq", split_axis=0, concat_axis=1, tiled=True
    ).reshape(clip_latents.shape)
    upstream_adjoint = lax.all_to_all(
        adjoint_seed.reshape(frames, places, channels),
        "seq",
        split_axis=1,
        concat_axis=0,
        tiled=True,
    )
    feature_adjoint, triple_projector_adjoint, emitted_adjoint = temporal_mixing_reverse(
        placed_features,
        upstream_adjoint,
        standardised_tokens,
        mapped_tokens,
        softmax_blend,
        triple_projector,
        exit_projector,
        logit_scaling,
    )
    back_frames = lax.all_to_all(feature_adjoint, "seq", split_axis=0, concat_axis=1, tiled=True)
    d_source, grad_conv = spatial_backward(
        back_frames.reshape(frames * places, channels),
        patches,
        pull_act,
        kernel_matrix,
        frames,
        height,
        breadth,
    )
    d_video = d_source.reshape(clip_latents.shape)
    factor = 1.0 / math.sqrt(lax.axis_size("grp") * lax.axis_size("seq") * frames * places)
    g_conv, g_qkv, g_out = tree_all_reduce(
        (grad_conv * factor, triple_projector_adjoint * factor, emitted_adjoint * factor)
    )
    return (output, d_video, g_conv, g_qkv, g_out)


def solution(mesh):
    return jax.shard_map(
        body,
        mesh=mesh,
        in_specs=(P("grp", "seq", None, None), P("grp", "seq", None, None), P(), P(), P(), P()),
        out_specs=(P("grp", "seq", None, None), P("grp", "seq", None, None), P(), P(), P()),
        check_vma=False,
    )
```

```python
import math

import jax
import jax.numpy as jnp
from jax import lax
from jax.sharding import PartitionSpec as P

HEAD_DIM = 64
GROUPS = 32


def group_act(widened):
    frames, height, breadth, channels = widened.shape
    span = channels // GROUPS
    count = height * breadth * span
    tokens = widened.reshape(frames, height * breadth, channels)

    def per_group(column_sums):
        totals = column_sums.reshape(frames, GROUPS, span).sum(axis=-1) / count
        return jnp.repeat(totals, span, axis=-1)[:, None, :]

    centre = per_group(jnp.sum(tokens, axis=1))
    shifted = tokens - centre
    spread = per_group(jnp.sum(jnp.square(shifted), axis=1))
    normed = shifted * lax.rsqrt(spread + 1e-05)
    return jax.nn.silu(normed).reshape(frames, height, breadth, channels)


def make_patches(active):
    frames, height, breadth, channels = active.shape
    padded = jnp.pad(active, ((0, 0), (1, 1), (1, 1), (0, 0)))
    pieces = [
        padded[:, down_step : down_step + height, side_step : side_step + breadth, :]
        for down_step in range(3)
        for side_step in range(3)
    ]
    return jnp.concatenate(pieces, axis=-1).reshape(frames * height * breadth, 9 * channels)


def fold_patches(columns, frames, height, breadth):
    channels = columns.shape[-1] // 9
    pieces = columns.reshape(frames, height, breadth, 9, channels)
    totals = jnp.zeros((frames, height + 2, breadth + 2, channels), jnp.float32)
    for down_step in range(3):
        for side_step in range(3):
            shifted = pieces[:, :, :, down_step * 3 + side_step, :]
            totals = totals + jnp.pad(
                shifted, ((0, 0), (down_step, 2 - down_step), (side_step, 2 - side_step), (0, 0))
            )
    return totals[:, 1 : height + 1, 1 : breadth + 1, :]


def layer_norm(widened):
    centre = jnp.mean(widened, axis=-1, keepdims=True)
    spread = jnp.mean(jnp.square(widened - centre), axis=-1, keepdims=True)
    return (widened - centre) * lax.rsqrt(spread + 1e-05)


def temporal_mixing(mapped_tokens, logit_scaling):
    frames, places, triple = mapped_tokens.shape
    channels = triple // 3
    head_count = channels // HEAD_DIM
    pieces = mapped_tokens.reshape(frames, places, 3, head_count, HEAD_DIM)
    query = pieces[:, :, 0]
    keys = pieces[:, :, 1]
    values = pieces[:, :, 2].astype(jnp.bfloat16)
    query = (
        query
        * lax.rsqrt(jnp.sum(query * query, axis=-1, keepdims=True) + 1e-06)
        * logit_scaling[:, None]
    ).astype(jnp.bfloat16)
    keys = (keys * lax.rsqrt(jnp.sum(keys * keys, axis=-1, keepdims=True) + 1e-06)).astype(
        jnp.bfloat16
    )
    scores = jnp.einsum("flhd,glhd->lhfg", query, keys, preferred_element_type=jnp.float32)
    weights = jnp.exp(scores)
    weights = (weights / jnp.sum(weights, axis=-1, keepdims=True)).astype(jnp.bfloat16)
    blend = jnp.einsum("lhfg,glhd->flhd", weights, values, preferred_element_type=jnp.float32)
    return blend.reshape(frames, places, channels)


def contract_rows(left, right):
    return lax.dot_general(
        left, right, (((0,), (0,)), ((), ())), preferred_element_type=jnp.float32
    )


def spatial_forward(source, kernel_matrix):
    frames, height, breadth, channels = source.shape
    widened = source.astype(jnp.float32)
    active, pull_act = jax.vjp(group_act, widened)
    patches = make_patches(active.astype(jnp.bfloat16))
    convolved = jnp.dot(patches, kernel_matrix, preferred_element_type=jnp.float32)
    latent_features = (widened.reshape(frames * height * breadth, channels) + convolved).astype(
        jnp.bfloat16
    )
    return (latent_features, patches, pull_act)


def spatial_backward(upstream_adjoint, patches, pull_act, kernel_matrix, frames, height, breadth):
    channels = upstream_adjoint.shape[-1]
    grad_conv = contract_rows(patches, upstream_adjoint)
    columns = jnp.dot(upstream_adjoint, kernel_matrix.T, preferred_element_type=jnp.float32)
    d_active = fold_patches(columns, frames, height, breadth)
    d_source = pull_act(d_active)[0]
    section_outcome = (
        upstream_adjoint.astype(jnp.float32).reshape(frames, height, breadth, channels) + d_source
    ).astype(jnp.bfloat16)
    return (section_outcome, grad_conv)


def temporal_mixing_apply(latent_features, triple_projector, exit_projector, logit_scaling):
    frames, places, channels = latent_features.shape
    widened = latent_features.astype(jnp.float32)
    standardised_tokens = layer_norm(widened).astype(jnp.bfloat16)
    mapped_tokens = jnp.dot(
        standardised_tokens.reshape(frames * places, channels),
        triple_projector,
        preferred_element_type=jnp.float32,
    ).reshape(frames, places, 3 * channels)
    softmax_blend = temporal_mixing(mapped_tokens, logit_scaling).astype(jnp.bfloat16)
    branch = jnp.dot(
        softmax_blend.reshape(frames * places, channels),
        exit_projector,
        preferred_element_type=jnp.float32,
    )
    section_outcome = (widened + branch.reshape(frames, places, channels)).astype(jnp.bfloat16)
    return (section_outcome, standardised_tokens, mapped_tokens, softmax_blend)


def temporal_mixing_reverse(
    latent_features,
    upstream_adjoint,
    standardised_tokens,
    mapped_tokens,
    softmax_blend,
    triple_projector,
    exit_projector,
    logit_scaling,
):
    frames, places, channels = latent_features.shape
    rows_cot = upstream_adjoint.reshape(frames * places, channels)
    emitted_adjoint = contract_rows(softmax_blend.reshape(frames * places, channels), rows_cot)
    d_mixture = jnp.dot(rows_cot, exit_projector.T, preferred_element_type=jnp.float32).astype(
        jnp.bfloat16
    )
    discarded_item, temporal_mixing_adjoint = jax.vjp(
        lambda entry_tensor: temporal_mixing(entry_tensor, logit_scaling), mapped_tokens
    )
    d_projected = temporal_mixing_adjoint(
        d_mixture.astype(jnp.float32).reshape(frames, places, channels)
    )[0].astype(jnp.bfloat16)
    rows_proj = d_projected.reshape(frames * places, 3 * channels)
    triple_projector_adjoint = contract_rows(
        standardised_tokens.reshape(frames * places, channels), rows_proj
    )
    d_normed = jnp.dot(rows_proj, triple_projector.T, preferred_element_type=jnp.float32).reshape(
        frames, places, channels
    )
    discarded_item, pull_norm = jax.vjp(layer_norm, latent_features.astype(jnp.float32))
    d_layer = pull_norm(d_normed)[0].astype(jnp.bfloat16)
    feature_adjoint = (upstream_adjoint.astype(jnp.float32) + d_layer.astype(jnp.float32)).astype(
        jnp.bfloat16
    )
    return (feature_adjoint, triple_projector_adjoint, emitted_adjoint)


CORE_BITS = (0,)
AXIS_BITS = {"x": (3, 6), "y": (4, 5), "z": (1, 2)}
ROUNDS = (("x", "z", "y"), ("z", "y", "x"))


def tree_all_reduce(parts):
    devices = lax.axis_size("grp") * lax.axis_size("seq")
    lead = parts[0]
    lead_rows = -(-lead.shape[0] // (devices * 8)) * 8 * devices
    lead_block = jnp.pad(lead, ((0, lead_rows - lead.shape[0]), (0, 0)))
    rest = jnp.concatenate([part.reshape(-1) for part in parts[1:]])
    rows = -(-rest.size // (devices * 128 * 8)) * 8
    rest = jnp.pad(rest, (0, devices * rows * 128 - rest.size))
    blocks = [lead_block.reshape(devices, -1, lead.shape[1]), rest.reshape(devices, rows, 128)]
    me = lax.axis_index("grp") * lax.axis_size("seq") + lax.axis_index("seq")
    core = me & 1
    rounds = [(CORE_BITS, CORE_BITS)] + [
        (AXIS_BITS[first], AXIS_BITS[second]) for first, second in zip(*ROUNDS)
    ]

    def flip(j, bits, mask):
        for place, bit in enumerate(bits):
            if (mask >> place) & 1:
                j ^= 1 << bit
        return j

    def position(bits):
        return sum(((me >> bit) & 1) << place for place, bit in enumerate(bits))

    def plan(choice):
        size = 1 << len(choice[0])
        spot = jnp.where(core == 0, position(choice[0]), position(choice[1]))
        perms = [
            [(j, flip(j, choice[j & 1], mask)) for j in range(devices)] for mask in range(1, size)
        ]
        return size, spot, perms

    for choice in rounds:
        size, spot, perms = plan(choice)
        piece = blocks[0].shape[0] // size
        totals = [lax.dynamic_slice_in_dim(block, spot * piece, piece, 0) for block in blocks]
        for mask, perm in zip(range(1, size), perms):
            sends = [
                lax.dynamic_slice_in_dim(block, (spot ^ mask) * piece, piece, 0).astype(jnp.bfloat16)
                for block in blocks
            ]
            gots = lax.ppermute(sends, ("grp", "seq"), perm)
            totals = [total + got.astype(jnp.float32) for total, got in zip(totals, gots)]
        blocks = totals
    blocks = [block.astype(jnp.bfloat16) for block in blocks]
    for choice in reversed(rounds):
        size, spot, perms = plan(choice)
        piece = blocks[0].shape[0]
        wholes = []
        for block in blocks:
            whole = jnp.zeros((size * piece,) + block.shape[1:], block.dtype)
            wholes.append(lax.dynamic_update_slice_in_dim(whole, block, spot * piece, 0))
        for mask, perm in zip(range(1, size), perms):
            gots = lax.ppermute(blocks, ("grp", "seq"), perm)
            wholes = [
                lax.dynamic_update_slice_in_dim(whole, got, (spot ^ mask) * piece, 0)
                for whole, got in zip(wholes, gots)
            ]
        blocks = wholes
    lead_sum = blocks[0].reshape(-1, lead.shape[1])[: lead.shape[0]].astype(jnp.float32)
    flat = blocks[1].reshape(-1).astype(jnp.float32)
    sums = [lead_sum]
    start = 0
    for part in parts[1:]:
        sums.append(flat[start : start + part.size].reshape(part.shape))
        start += part.size
    return tuple(sums)


def body(
    clip_latents, adjoint_seed, kernel_matrix, triple_projector, exit_projector, logit_scaling
):
    frames = clip_latents.shape[1]
    height = clip_latents.shape[2]
    channels = exit_projector.shape[0]
    breadth = clip_latents.shape[3] // channels
    places = height * breadth
    source = clip_latents.reshape(frames, height, breadth, channels)
    latent_features, patches, pull_act = spatial_forward(source, kernel_matrix)
    placed_features = lax.all_to_all(
        latent_features.reshape(frames, places, channels),
        "seq",
        split_axis=1,
        concat_axis=0,
        tiled=True,
    )
    section_outcome, standardised_tokens, mapped_tokens, softmax_blend = temporal_mixing_apply(
        placed_features, triple_projector, exit_projector, logit_scaling
    )
    output = lax.all_to_all(
        section_outcome, "seq", split_axis=0, concat_axis=1, tiled=True
    ).reshape(clip_latents.shape)
    upstream_adjoint = lax.all_to_all(
        adjoint_seed.reshape(frames, places, channels),
        "seq",
        split_axis=1,
        concat_axis=0,
        tiled=True,
    )
    feature_adjoint, triple_projector_adjoint, emitted_adjoint = temporal_mixing_reverse(
        placed_features,
        upstream_adjoint,
        standardised_tokens,
        mapped_tokens,
        softmax_blend,
        triple_projector,
        exit_projector,
        logit_scaling,
    )
    back_frames = lax.all_to_all(feature_adjoint, "seq", split_axis=0, concat_axis=1, tiled=True)
    d_source, grad_conv = spatial_backward(
        back_frames.reshape(frames * places, channels),
        patches,
        pull_act,
        kernel_matrix,
        frames,
        height,
        breadth,
    )
    d_video = d_source.reshape(clip_latents.shape)
    factor = 1.0 / math.sqrt(lax.axis_size("grp") * lax.axis_size("seq") * frames * places)
    g_conv, g_qkv, g_out = tree_all_reduce(
        (grad_conv * factor, triple_projector_adjoint * factor, emitted_adjoint * factor)
    )
    return (output, d_video, g_conv, g_qkv, g_out)


def solution(mesh):
    return jax.shard_map(
        body,
        mesh=mesh,
        in_specs=(P("grp", "seq", None, None), P("grp", "seq", None, None), P(), P(), P(), P()),
        out_specs=(P("grp", "seq", None, None), P("grp", "seq", None, None), P(), P(), P()),
        check_vma=False,
    )
```

```python
import math

import jax
import jax.numpy as jnp
from jax import lax
from jax.sharding import PartitionSpec as P

HEAD_DIM = 64
GROUPS = 32


def group_act(widened):
    frames, height, breadth, channels = widened.shape
    span = channels // GROUPS
    count = height * breadth * span
    tokens = widened.reshape(frames, height * breadth, channels)

    def per_group(column_sums):
        totals = column_sums.reshape(frames, GROUPS, span).sum(axis=-1) / count
        return jnp.repeat(totals, span, axis=-1)[:, None, :]

    centre = per_group(jnp.sum(tokens, axis=1))
    shifted = tokens - centre
    spread = per_group(jnp.sum(jnp.square(shifted), axis=1))
    normed = shifted * lax.rsqrt(spread + 1e-05)
    return jax.nn.silu(normed).reshape(frames, height, breadth, channels)


def make_patches(active):
    frames, height, breadth, channels = active.shape
    padded = jnp.pad(active, ((0, 0), (1, 1), (1, 1), (0, 0)))
    pieces = [
        padded[:, down_step : down_step + height, side_step : side_step + breadth, :]
        for down_step in range(3)
        for side_step in range(3)
    ]
    return jnp.concatenate(pieces, axis=-1).reshape(frames * height * breadth, 9 * channels)


def fold_patches(columns, frames, height, breadth):
    channels = columns.shape[-1] // 9
    pieces = columns.reshape(frames, height, breadth, 9, channels)
    totals = jnp.zeros((frames, height + 2, breadth + 2, channels), jnp.float32)
    for down_step in range(3):
        for side_step in range(3):
            shifted = pieces[:, :, :, down_step * 3 + side_step, :]
            totals = totals + jnp.pad(
                shifted, ((0, 0), (down_step, 2 - down_step), (side_step, 2 - side_step), (0, 0))
            )
    return totals[:, 1 : height + 1, 1 : breadth + 1, :]


def layer_norm(widened):
    centre = jnp.mean(widened, axis=-1, keepdims=True)
    spread = jnp.mean(jnp.square(widened - centre), axis=-1, keepdims=True)
    return (widened - centre) * lax.rsqrt(spread + 1e-05)


def temporal_mixing(mapped_tokens, logit_scaling):
    frames, places, triple = mapped_tokens.shape
    channels = triple // 3
    head_count = channels // HEAD_DIM
    pieces = mapped_tokens.reshape(frames, places, 3, head_count, HEAD_DIM)
    query = pieces[:, :, 0]
    keys = pieces[:, :, 1]
    values = pieces[:, :, 2].astype(jnp.bfloat16)
    query = (
        query
        * lax.rsqrt(jnp.sum(query * query, axis=-1, keepdims=True) + 1e-06)
        * logit_scaling[:, None]
    ).astype(jnp.bfloat16)
    keys = (keys * lax.rsqrt(jnp.sum(keys * keys, axis=-1, keepdims=True) + 1e-06)).astype(
        jnp.bfloat16
    )
    scores = jnp.einsum("flhd,glhd->lhfg", query, keys, preferred_element_type=jnp.float32)
    weights = jnp.exp(scores)
    weights = (weights / jnp.sum(weights, axis=-1, keepdims=True)).astype(jnp.bfloat16)
    blend = jnp.einsum("lhfg,glhd->flhd", weights, values, preferred_element_type=jnp.float32)
    return blend.reshape(frames, places, channels)


def contract_rows(left, right):
    return lax.dot_general(
        left, right, (((0,), (0,)), ((), ())), preferred_element_type=jnp.float32
    )


def spatial_forward(source, kernel_matrix):
    frames, height, breadth, channels = source.shape
    widened = source.astype(jnp.float32)
    active, pull_act = jax.vjp(group_act, widened)
    patches = make_patches(active.astype(jnp.bfloat16))
    convolved = jnp.dot(patches, kernel_matrix, preferred_element_type=jnp.float32)
    latent_features = (widened.reshape(frames * height * breadth, channels) + convolved).astype(
        jnp.bfloat16
    )
    return (latent_features, patches, pull_act)


def spatial_backward(upstream_adjoint, patches, pull_act, kernel_matrix, frames, height, breadth):
    channels = upstream_adjoint.shape[-1]
    grad_conv = contract_rows(patches, upstream_adjoint)
    columns = jnp.dot(upstream_adjoint, kernel_matrix.T, preferred_element_type=jnp.float32)
    d_active = fold_patches(columns, frames, height, breadth)
    d_source = pull_act(d_active)[0]
    section_outcome = (
        upstream_adjoint.astype(jnp.float32).reshape(frames, height, breadth, channels) + d_source
    ).astype(jnp.bfloat16)
    return (section_outcome, grad_conv)


def temporal_mixing_apply(latent_features, triple_projector, exit_projector, logit_scaling):
    frames, places, channels = latent_features.shape
    widened = latent_features.astype(jnp.float32)
    standardised_tokens = layer_norm(widened).astype(jnp.bfloat16)
    mapped_tokens = jnp.dot(
        standardised_tokens.reshape(frames * places, channels),
        triple_projector,
        preferred_element_type=jnp.float32,
    ).reshape(frames, places, 3 * channels)
    softmax_blend = temporal_mixing(mapped_tokens, logit_scaling).astype(jnp.bfloat16)
    branch = jnp.dot(
        softmax_blend.reshape(frames * places, channels),
        exit_projector,
        preferred_element_type=jnp.float32,
    )
    section_outcome = (widened + branch.reshape(frames, places, channels)).astype(jnp.bfloat16)
    return (section_outcome, standardised_tokens, mapped_tokens, softmax_blend)


def temporal_mixing_reverse(
    latent_features,
    upstream_adjoint,
    standardised_tokens,
    mapped_tokens,
    softmax_blend,
    triple_projector,
    exit_projector,
    logit_scaling,
):
    frames, places, channels = latent_features.shape
    rows_cot = upstream_adjoint.reshape(frames * places, channels)
    emitted_adjoint = contract_rows(softmax_blend.reshape(frames * places, channels), rows_cot)
    d_mixture = jnp.dot(rows_cot, exit_projector.T, preferred_element_type=jnp.float32).astype(
        jnp.bfloat16
    )
    discarded_item, temporal_mixing_adjoint = jax.vjp(
        lambda entry_tensor: temporal_mixing(entry_tensor, logit_scaling), mapped_tokens
    )
    d_projected = temporal_mixing_adjoint(
        d_mixture.astype(jnp.float32).reshape(frames, places, channels)
    )[0].astype(jnp.bfloat16)
    rows_proj = d_projected.reshape(frames * places, 3 * channels)
    triple_projector_adjoint = contract_rows(
        standardised_tokens.reshape(frames * places, channels), rows_proj
    )
    d_normed = jnp.dot(rows_proj, triple_projector.T, preferred_element_type=jnp.float32).reshape(
        frames, places, channels
    )
    discarded_item, pull_norm = jax.vjp(layer_norm, latent_features.astype(jnp.float32))
    d_layer = pull_norm(d_normed)[0].astype(jnp.bfloat16)
    feature_adjoint = (upstream_adjoint.astype(jnp.float32) + d_layer.astype(jnp.float32)).astype(
        jnp.bfloat16
    )
    return (feature_adjoint, triple_projector_adjoint, emitted_adjoint)


CORE_BITS = (0,)
AXIS_BITS = {"x": (3, 6), "y": (4, 5), "z": (1, 2)}
ROUNDS = (("x", "z", "y"), ("z", "y", "x"))


def tree_all_reduce(parts):
    devices = lax.axis_size("grp") * lax.axis_size("seq")
    flat = jnp.concatenate([part.reshape(-1) for part in parts])
    rows = -(-flat.size // (devices * 128 * 8)) * 8
    flat = jnp.pad(flat, (0, devices * rows * 128 - flat.size))
    block = flat.reshape(devices, rows, 128)
    me = lax.axis_index("grp") * lax.axis_size("seq") + lax.axis_index("seq")
    core = me & 1
    rounds = [(CORE_BITS, CORE_BITS)] + [
        (AXIS_BITS[first], AXIS_BITS[second]) for first, second in zip(*ROUNDS)
    ]

    def flip(j, bits, mask):
        for place, bit in enumerate(bits):
            if (mask >> place) & 1:
                j ^= 1 << bit
        return j

    def position(bits):
        return sum(((me >> bit) & 1) << place for place, bit in enumerate(bits))

    def plan(choice):
        size = 1 << len(choice[0])
        spot = jnp.where(core == 0, position(choice[0]), position(choice[1]))
        perms = [
            [(j, flip(j, choice[j & 1], mask)) for j in range(devices)] for mask in range(1, size)
        ]
        return size, spot, perms

    for choice in rounds:
        size, spot, perms = plan(choice)
        piece = block.shape[0] // size
        total = lax.dynamic_slice_in_dim(block, spot * piece, piece, 0)
        for mask, perm in zip(range(1, size), perms):
            send = lax.dynamic_slice_in_dim(block, (spot ^ mask) * piece, piece, 0)
            got = lax.ppermute(send.astype(jnp.bfloat16), ("grp", "seq"), perm)
            total = total + got.astype(jnp.float32)
        block = total
    block = block.astype(jnp.bfloat16)
    for choice in reversed(rounds):
        size, spot, perms = plan(choice)
        piece = block.shape[0]
        whole = jnp.zeros((size * piece,) + block.shape[1:], block.dtype)
        whole = lax.dynamic_update_slice_in_dim(whole, block, spot * piece, 0)
        for mask, perm in zip(range(1, size), perms):
            got = lax.ppermute(block, ("grp", "seq"), perm)
            whole = lax.dynamic_update_slice_in_dim(whole, got, (spot ^ mask) * piece, 0)
        block = whole
    flat = block.reshape(-1).astype(jnp.float32)
    sums = []
    start = 0
    for part in parts:
        sums.append(flat[start : start + part.size].reshape(part.shape))
        start += part.size
    return tuple(sums)


def body(
    clip_latents, adjoint_seed, kernel_matrix, triple_projector, exit_projector, logit_scaling
):
    frames = clip_latents.shape[1]
    height = clip_latents.shape[2]
    channels = exit_projector.shape[0]
    breadth = clip_latents.shape[3] // channels
    places = height * breadth
    source = clip_latents.reshape(frames, height, breadth, channels)
    latent_features, patches, pull_act = spatial_forward(source, kernel_matrix)
    placed_features = lax.all_to_all(
        latent_features.reshape(frames, places, channels),
        "seq",
        split_axis=1,
        concat_axis=0,
        tiled=True,
    )
    section_outcome, standardised_tokens, mapped_tokens, softmax_blend = temporal_mixing_apply(
        placed_features, triple_projector, exit_projector, logit_scaling
    )
    output = lax.all_to_all(
        section_outcome, "seq", split_axis=0, concat_axis=1, tiled=True
    ).reshape(clip_latents.shape)
    upstream_adjoint = lax.all_to_all(
        adjoint_seed.reshape(frames, places, channels),
        "seq",
        split_axis=1,
        concat_axis=0,
        tiled=True,
    )
    feature_adjoint, triple_projector_adjoint, emitted_adjoint = temporal_mixing_reverse(
        placed_features,
        upstream_adjoint,
        standardised_tokens,
        mapped_tokens,
        softmax_blend,
        triple_projector,
        exit_projector,
        logit_scaling,
    )
    back_frames = lax.all_to_all(feature_adjoint, "seq", split_axis=0, concat_axis=1, tiled=True)
    d_source, grad_conv = spatial_backward(
        back_frames.reshape(frames * places, channels),
        patches,
        pull_act,
        kernel_matrix,
        frames,
        height,
        breadth,
    )
    d_video = d_source.reshape(clip_latents.shape)
    factor = 1.0 / math.sqrt(lax.axis_size("grp") * lax.axis_size("seq") * frames * places)
    g_conv_t, g_qkv, g_out = tree_all_reduce(
        (grad_conv.T * factor, triple_projector_adjoint * factor, emitted_adjoint * factor)
    )
    g_conv = g_conv_t.T
    return (output, d_video, g_conv, g_qkv, g_out)


def solution(mesh):
    return jax.shard_map(
        body,
        mesh=mesh,
        in_specs=(P("grp", "seq", None, None), P("grp", "seq", None, None), P(), P(), P(), P()),
        out_specs=(P("grp", "seq", None, None), P("grp", "seq", None, None), P(), P(), P()),
        check_vma=False,
    )
```

```python
import math

import jax
import jax.numpy as jnp
from jax import lax
from jax.sharding import PartitionSpec as P

HEAD_DIM = 64
GROUPS = 32


def group_act(widened):
    frames, height, breadth, channels = widened.shape
    span = channels // GROUPS
    count = height * breadth * span
    tokens = widened.reshape(frames, height * breadth, channels)

    def per_group(column_sums):
        totals = column_sums.reshape(frames, GROUPS, span).sum(axis=-1) / count
        return jnp.repeat(totals, span, axis=-1)[:, None, :]

    centre = per_group(jnp.sum(tokens, axis=1))
    shifted = tokens - centre
    spread = per_group(jnp.sum(jnp.square(shifted), axis=1))
    normed = shifted * lax.rsqrt(spread + 1e-05)
    return jax.nn.silu(normed).reshape(frames, height, breadth, channels)


def make_patches(active):
    frames, height, breadth, channels = active.shape
    padded = jnp.pad(active, ((0, 0), (1, 1), (1, 1), (0, 0)))
    pieces = [
        padded[:, down_step : down_step + height, side_step : side_step + breadth, :]
        for down_step in range(3)
        for side_step in range(3)
    ]
    return jnp.concatenate(pieces, axis=-1).reshape(frames * height * breadth, 9 * channels)


def fold_patches(columns, frames, height, breadth):
    channels = columns.shape[-1] // 9
    pieces = columns.reshape(frames, height, breadth, 9, channels)
    totals = jnp.zeros((frames, height + 2, breadth + 2, channels), jnp.float32)
    for down_step in range(3):
        for side_step in range(3):
            shifted = pieces[:, :, :, down_step * 3 + side_step, :]
            totals = totals + jnp.pad(
                shifted, ((0, 0), (down_step, 2 - down_step), (side_step, 2 - side_step), (0, 0))
            )
    return totals[:, 1 : height + 1, 1 : breadth + 1, :]


def layer_norm(widened):
    centre = jnp.mean(widened, axis=-1, keepdims=True)
    spread = jnp.mean(jnp.square(widened - centre), axis=-1, keepdims=True)
    return (widened - centre) * lax.rsqrt(spread + 1e-05)


def temporal_mixing(mapped_tokens, logit_scaling):
    query, keys, values = mapped_tokens
    frames, places, channels = query.shape
    head_count = channels // HEAD_DIM
    member = jnp.arange(channels)[None, :] // HEAD_DIM == jnp.arange(head_count)[:, None]

    def per_head(tokens):
        return jnp.sum(tokens.reshape(frames, places, head_count, HEAD_DIM), axis=-1)

    def per_channel(heads):
        return jnp.repeat(heads, HEAD_DIM, axis=-1)

    query = (
        query
        * per_channel(lax.rsqrt(per_head(query * query) + 1e-06))
        * per_channel(jnp.broadcast_to(logit_scaling, (frames, places, head_count)))
    ).astype(jnp.bfloat16)
    keys = (keys * per_channel(lax.rsqrt(per_head(keys * keys) + 1e-06))).astype(jnp.bfloat16)
    values = values.astype(jnp.bfloat16)
    picked = query[None] * member[:, None, None, :].astype(jnp.bfloat16)
    scores = jnp.einsum("hflc,glc->lhfg", picked, keys, preferred_element_type=jnp.float32)
    weights = jnp.exp(scores)
    weights = (weights / jnp.sum(weights, axis=-1, keepdims=True)).astype(jnp.bfloat16)
    mixed = jnp.einsum("lhfg,glc->hflc", weights, values, preferred_element_type=jnp.float32)
    return jnp.sum(mixed * member[:, None, None, :].astype(jnp.float32), axis=0)


def contract_rows(left, right):
    return lax.dot_general(
        left, right, (((0,), (0,)), ((), ())), preferred_element_type=jnp.float32
    )


def spatial_forward(source, kernel_matrix):
    frames, height, breadth, channels = source.shape
    widened = source.astype(jnp.float32)
    active, pull_act = jax.vjp(group_act, widened)
    patches = make_patches(active.astype(jnp.bfloat16))
    convolved = jnp.dot(patches, kernel_matrix, preferred_element_type=jnp.float32)
    latent_features = (widened.reshape(frames * height * breadth, channels) + convolved).astype(
        jnp.bfloat16
    )
    return (latent_features, patches, pull_act)


def spatial_backward(upstream_adjoint, patches, pull_act, kernel_matrix, frames, height, breadth):
    channels = upstream_adjoint.shape[-1]
    grad_conv = contract_rows(patches, upstream_adjoint)
    columns = jnp.dot(upstream_adjoint, kernel_matrix.T, preferred_element_type=jnp.float32)
    d_active = fold_patches(columns, frames, height, breadth)
    d_source = pull_act(d_active)[0]
    section_outcome = (
        upstream_adjoint.astype(jnp.float32).reshape(frames, height, breadth, channels) + d_source
    ).astype(jnp.bfloat16)
    return (section_outcome, grad_conv)


def temporal_mixing_apply(latent_features, triple_projector, exit_projector, logit_scaling):
    frames, places, channels = latent_features.shape
    widened = latent_features.astype(jnp.float32)
    standardised_tokens = layer_norm(widened).astype(jnp.bfloat16)
    mapped_tokens = tuple(
        jnp.dot(
            standardised_tokens.reshape(frames * places, channels),
            triple_projector[:, part * channels : (part + 1) * channels],
            preferred_element_type=jnp.float32,
        ).reshape(frames, places, channels)
        for part in range(3)
    )
    softmax_blend = temporal_mixing(mapped_tokens, logit_scaling).astype(jnp.bfloat16)
    branch = jnp.dot(
        softmax_blend.reshape(frames * places, channels),
        exit_projector,
        preferred_element_type=jnp.float32,
    )
    section_outcome = (widened + branch.reshape(frames, places, channels)).astype(jnp.bfloat16)
    return (section_outcome, standardised_tokens, mapped_tokens, softmax_blend)


def temporal_mixing_reverse(
    latent_features,
    upstream_adjoint,
    standardised_tokens,
    mapped_tokens,
    softmax_blend,
    triple_projector,
    exit_projector,
    logit_scaling,
):
    frames, places, channels = latent_features.shape
    rows_cot = upstream_adjoint.reshape(frames * places, channels)
    emitted_adjoint = contract_rows(softmax_blend.reshape(frames * places, channels), rows_cot)
    d_mixture = jnp.dot(rows_cot, exit_projector.T, preferred_element_type=jnp.float32).astype(
        jnp.bfloat16
    )
    discarded_item, temporal_mixing_adjoint = jax.vjp(
        lambda entry_tensor: temporal_mixing(entry_tensor, logit_scaling), mapped_tokens
    )
    d_projected = [
        part.astype(jnp.bfloat16).reshape(frames * places, channels)
        for part in temporal_mixing_adjoint(
            d_mixture.astype(jnp.float32).reshape(frames, places, channels)
        )[0]
    ]
    rows_normed = standardised_tokens.reshape(frames * places, channels)
    triple_projector_adjoint = jnp.concatenate(
        [contract_rows(rows_normed, part) for part in d_projected], axis=1
    )
    d_normed = sum(
        jnp.dot(
            part,
            triple_projector[:, index * channels : (index + 1) * channels].T,
            preferred_element_type=jnp.float32,
        )
        for index, part in enumerate(d_projected)
    ).reshape(frames, places, channels)
    discarded_item, pull_norm = jax.vjp(layer_norm, latent_features.astype(jnp.float32))
    d_layer = pull_norm(d_normed)[0].astype(jnp.bfloat16)
    feature_adjoint = (upstream_adjoint.astype(jnp.float32) + d_layer.astype(jnp.float32)).astype(
        jnp.bfloat16
    )
    return (feature_adjoint, triple_projector_adjoint, emitted_adjoint)


CORE_BITS = (0,)
AXIS_BITS = {"x": (3, 6), "y": (4, 5), "z": (1, 2)}
ROUNDS = (("x", "z", "y"), ("z", "y", "x"))


def tree_all_reduce(parts):
    devices = lax.axis_size("grp") * lax.axis_size("seq")
    flat = jnp.concatenate([part.reshape(-1) for part in parts])
    rows = -(-flat.size // (devices * 128 * 8)) * 8
    flat = jnp.pad(flat, (0, devices * rows * 128 - flat.size))
    block = flat.reshape(devices, rows, 128)
    me = lax.axis_index("grp") * lax.axis_size("seq") + lax.axis_index("seq")
    core = me & 1
    rounds = [(CORE_BITS, CORE_BITS)] + [
        (AXIS_BITS[first], AXIS_BITS[second]) for first, second in zip(*ROUNDS)
    ]

    def flip(j, bits, mask):
        for place, bit in enumerate(bits):
            if (mask >> place) & 1:
                j ^= 1 << bit
        return j

    def position(bits):
        return sum(((me >> bit) & 1) << place for place, bit in enumerate(bits))

    def plan(choice):
        size = 1 << len(choice[0])
        spot = jnp.where(core == 0, position(choice[0]), position(choice[1]))
        perms = [
            [(j, flip(j, choice[j & 1], mask)) for j in range(devices)] for mask in range(1, size)
        ]
        return size, spot, perms

    for choice in rounds:
        size, spot, perms = plan(choice)
        piece = block.shape[0] // size
        total = lax.dynamic_slice_in_dim(block, spot * piece, piece, 0)
        for mask, perm in zip(range(1, size), perms):
            send = lax.dynamic_slice_in_dim(block, (spot ^ mask) * piece, piece, 0)
            got = lax.ppermute(send.astype(jnp.bfloat16), ("grp", "seq"), perm)
            total = total + got.astype(jnp.float32)
        block = total
    block = block.astype(jnp.bfloat16)
    for choice in reversed(rounds):
        size, spot, perms = plan(choice)
        piece = block.shape[0]
        whole = jnp.zeros((size * piece,) + block.shape[1:], block.dtype)
        whole = lax.dynamic_update_slice_in_dim(whole, block, spot * piece, 0)
        for mask, perm in zip(range(1, size), perms):
            got = lax.ppermute(block, ("grp", "seq"), perm)
            whole = lax.dynamic_update_slice_in_dim(whole, got, (spot ^ mask) * piece, 0)
        block = whole
    flat = block.reshape(-1).astype(jnp.float32)
    sums = []
    start = 0
    for part in parts:
        sums.append(flat[start : start + part.size].reshape(part.shape))
        start += part.size
    return tuple(sums)


def body(
    clip_latents, adjoint_seed, kernel_matrix, triple_projector, exit_projector, logit_scaling
):
    frames = clip_latents.shape[1]
    height = clip_latents.shape[2]
    channels = exit_projector.shape[0]
    breadth = clip_latents.shape[3] // channels
    places = height * breadth
    source = clip_latents.reshape(frames, height, breadth, channels)
    latent_features, patches, pull_act = spatial_forward(source, kernel_matrix)
    placed_features = lax.all_to_all(
        latent_features.reshape(frames, places, channels),
        "seq",
        split_axis=1,
        concat_axis=0,
        tiled=True,
    )
    section_outcome, standardised_tokens, mapped_tokens, softmax_blend = temporal_mixing_apply(
        placed_features, triple_projector, exit_projector, logit_scaling
    )
    output = lax.all_to_all(
        section_outcome, "seq", split_axis=0, concat_axis=1, tiled=True
    ).reshape(clip_latents.shape)
    upstream_adjoint = lax.all_to_all(
        adjoint_seed.reshape(frames, places, channels),
        "seq",
        split_axis=1,
        concat_axis=0,
        tiled=True,
    )
    feature_adjoint, triple_projector_adjoint, emitted_adjoint = temporal_mixing_reverse(
        placed_features,
        upstream_adjoint,
        standardised_tokens,
        mapped_tokens,
        softmax_blend,
        triple_projector,
        exit_projector,
        logit_scaling,
    )
    back_frames = lax.all_to_all(feature_adjoint, "seq", split_axis=0, concat_axis=1, tiled=True)
    d_source, grad_conv = spatial_backward(
        back_frames.reshape(frames * places, channels),
        patches,
        pull_act,
        kernel_matrix,
        frames,
        height,
        breadth,
    )
    d_video = d_source.reshape(clip_latents.shape)
    factor = 1.0 / math.sqrt(lax.axis_size("grp") * lax.axis_size("seq") * frames * places)
    g_conv_t, g_qkv, g_out = tree_all_reduce(
        (grad_conv.T * factor, triple_projector_adjoint * factor, emitted_adjoint * factor)
    )
    g_conv = g_conv_t.T
    return (output, d_video, g_conv, g_qkv, g_out)


def solution(mesh):
    return jax.shard_map(
        body,
        mesh=mesh,
        in_specs=(P("grp", "seq", None, None), P("grp", "seq", None, None), P(), P(), P(), P()),
        out_specs=(P("grp", "seq", None, None), P("grp", "seq", None, None), P(), P(), P()),
        check_vma=False,
    )
```

```python
import math

import jax
import jax.numpy as jnp
from jax import lax
from jax.sharding import PartitionSpec as P

HEAD_DIM = 64
GROUPS = 32


def group_act(widened):
    frames, height, breadth, channels = widened.shape
    span = channels // GROUPS
    count = height * breadth * span
    tokens = widened.reshape(frames, height * breadth, channels)

    def per_group(column_sums):
        totals = column_sums.reshape(frames, GROUPS, span).sum(axis=-1) / count
        return jnp.repeat(totals, span, axis=-1)[:, None, :]

    centre = per_group(jnp.sum(tokens, axis=1))
    shifted = tokens - centre
    spread = per_group(jnp.sum(jnp.square(shifted), axis=1))
    normed = shifted * lax.rsqrt(spread + 1e-05)
    return jax.nn.silu(normed).reshape(frames, height, breadth, channels)


def make_patches(active):
    frames, height, breadth, channels = active.shape
    padded = jnp.pad(active, ((0, 0), (1, 1), (1, 1), (0, 0)))
    pieces = [
        padded[:, down_step : down_step + height, side_step : side_step + breadth, :]
        for down_step in range(3)
        for side_step in range(3)
    ]
    return jnp.concatenate(pieces, axis=-1).reshape(frames * height * breadth, 9 * channels)


def fold_patches(columns, frames, height, breadth):
    channels = columns.shape[-1] // 9
    pieces = columns.reshape(frames, height, breadth, 9, channels)
    totals = jnp.zeros((frames, height + 2, breadth + 2, channels), jnp.float32)
    for down_step in range(3):
        for side_step in range(3):
            shifted = pieces[:, :, :, down_step * 3 + side_step, :]
            totals = totals + jnp.pad(
                shifted, ((0, 0), (down_step, 2 - down_step), (side_step, 2 - side_step), (0, 0))
            )
    return totals[:, 1 : height + 1, 1 : breadth + 1, :]


def layer_norm(widened):
    centre = jnp.mean(widened, axis=-1, keepdims=True)
    spread = jnp.mean(jnp.square(widened - centre), axis=-1, keepdims=True)
    return (widened - centre) * lax.rsqrt(spread + 1e-05)


def temporal_mixing(mapped_tokens, logit_scaling):
    frames, places, triple = mapped_tokens.shape
    channels = triple // 3
    head_count = channels // HEAD_DIM
    pieces = mapped_tokens.reshape(frames, places, 3, head_count, HEAD_DIM)
    query = pieces[:, :, 0]
    keys = pieces[:, :, 1]
    values = pieces[:, :, 2].astype(jnp.bfloat16)
    query = (
        query
        * lax.rsqrt(jnp.sum(query * query, axis=-1, keepdims=True) + 1e-06)
        * logit_scaling[:, None]
    ).astype(jnp.bfloat16)
    keys = (keys * lax.rsqrt(jnp.sum(keys * keys, axis=-1, keepdims=True) + 1e-06)).astype(
        jnp.bfloat16
    )
    scores = jnp.einsum("flhd,glhd->lhfg", query, keys, preferred_element_type=jnp.float32)
    weights = jnp.exp(scores)
    weights = (weights / jnp.sum(weights, axis=-1, keepdims=True)).astype(jnp.bfloat16)
    blend = jnp.einsum("lhfg,glhd->flhd", weights, values, preferred_element_type=jnp.float32)
    return blend.reshape(frames, places, channels)


def contract_rows(left, right):
    return lax.dot_general(
        left, right, (((0,), (0,)), ((), ())), preferred_element_type=jnp.float32
    )


def spatial_conv(tokens, kernel):
    return lax.conv_general_dilated(
        tokens,
        kernel,
        window_strides=(1, 1),
        padding=((1, 1), (1, 1)),
        dimension_numbers=("NHWC", "HWIO", "NHWC"),
        preferred_element_type=jnp.float32,
    )


def spatial_forward(source, kernel_matrix):
    frames, height, breadth, channels = source.shape
    widened = source.astype(jnp.float32)
    active, pull_act = jax.vjp(group_act, widened)
    active = active.astype(jnp.bfloat16)
    convolved = spatial_conv(active, kernel_matrix.reshape(3, 3, channels, channels))
    latent_features = (widened + convolved).astype(jnp.bfloat16)
    return (latent_features.reshape(frames * height * breadth, channels), active, pull_act)


def spatial_backward(upstream_adjoint, active, pull_act, kernel_matrix, frames, height, breadth):
    channels = upstream_adjoint.shape[-1]
    states_adjoint = upstream_adjoint.reshape(frames, height, breadth, channels)
    padded = jnp.pad(active, ((0, 0), (1, 1), (1, 1), (0, 0)))
    taps = lax.conv_general_dilated(
        padded,
        states_adjoint,
        window_strides=(1, 1),
        padding="VALID",
        dimension_numbers=("CHWN", "IHWO", "NHWC"),
        preferred_element_type=jnp.float32,
    )
    grad_conv = jnp.transpose(taps, (1, 2, 0, 3)).reshape(9 * channels, channels)
    flipped = jnp.transpose(kernel_matrix.reshape(3, 3, channels, channels)[::-1, ::-1], (0, 1, 3, 2))
    d_active = spatial_conv(states_adjoint, flipped)
    d_source = pull_act(d_active)[0]
    section_outcome = (states_adjoint.astype(jnp.float32) + d_source).astype(jnp.bfloat16)
    return (section_outcome, grad_conv)


def temporal_mixing_apply(latent_features, triple_projector, exit_projector, logit_scaling):
    frames, places, channels = latent_features.shape
    widened = latent_features.astype(jnp.float32)
    standardised_tokens = layer_norm(widened).astype(jnp.bfloat16)
    mapped_tokens = jnp.dot(
        standardised_tokens.reshape(frames * places, channels),
        triple_projector,
        preferred_element_type=jnp.float32,
    ).reshape(frames, places, 3 * channels)
    softmax_blend = temporal_mixing(mapped_tokens, logit_scaling).astype(jnp.bfloat16)
    branch = jnp.dot(
        softmax_blend.reshape(frames * places, channels),
        exit_projector,
        preferred_element_type=jnp.float32,
    )
    section_outcome = (widened + branch.reshape(frames, places, channels)).astype(jnp.bfloat16)
    return (section_outcome, standardised_tokens, mapped_tokens, softmax_blend)


def temporal_mixing_reverse(
    latent_features,
    upstream_adjoint,
    standardised_tokens,
    mapped_tokens,
    softmax_blend,
    triple_projector,
    exit_projector,
    logit_scaling,
):
    frames, places, channels = latent_features.shape
    rows_cot = upstream_adjoint.reshape(frames * places, channels)
    emitted_adjoint = contract_rows(softmax_blend.reshape(frames * places, channels), rows_cot)
    d_mixture = jnp.dot(rows_cot, exit_projector.T, preferred_element_type=jnp.float32).astype(
        jnp.bfloat16
    )
    discarded_item, temporal_mixing_adjoint = jax.vjp(
        lambda entry_tensor: temporal_mixing(entry_tensor, logit_scaling), mapped_tokens
    )
    d_projected = temporal_mixing_adjoint(
        d_mixture.astype(jnp.float32).reshape(frames, places, channels)
    )[0].astype(jnp.bfloat16)
    rows_proj = d_projected.reshape(frames * places, 3 * channels)
    triple_projector_adjoint = contract_rows(
        standardised_tokens.reshape(frames * places, channels), rows_proj
    )
    d_normed = jnp.dot(rows_proj, triple_projector.T, preferred_element_type=jnp.float32).reshape(
        frames, places, channels
    )
    discarded_item, pull_norm = jax.vjp(layer_norm, latent_features.astype(jnp.float32))
    d_layer = pull_norm(d_normed)[0].astype(jnp.bfloat16)
    feature_adjoint = (upstream_adjoint.astype(jnp.float32) + d_layer.astype(jnp.float32)).astype(
        jnp.bfloat16
    )
    return (feature_adjoint, triple_projector_adjoint, emitted_adjoint)


CORE_BITS = (0,)
AXIS_BITS = {"x": (3, 6), "y": (4, 5), "z": (1, 2)}
ROUNDS = (("x", "z", "y"), ("z", "y", "x"))


def tree_all_reduce(parts):
    devices = lax.axis_size("grp") * lax.axis_size("seq")
    flat = jnp.concatenate([part.reshape(-1) for part in parts])
    rows = -(-flat.size // (devices * 128 * 8)) * 8
    flat = jnp.pad(flat, (0, devices * rows * 128 - flat.size))
    block = flat.reshape(devices, rows, 128)
    me = lax.axis_index("grp") * lax.axis_size("seq") + lax.axis_index("seq")
    core = me & 1
    rounds = [(CORE_BITS, CORE_BITS)] + [
        (AXIS_BITS[first], AXIS_BITS[second]) for first, second in zip(*ROUNDS)
    ]

    def flip(j, bits, mask):
        for place, bit in enumerate(bits):
            if (mask >> place) & 1:
                j ^= 1 << bit
        return j

    def position(bits):
        return sum(((me >> bit) & 1) << place for place, bit in enumerate(bits))

    def plan(choice):
        size = 1 << len(choice[0])
        spot = jnp.where(core == 0, position(choice[0]), position(choice[1]))
        perms = [
            [(j, flip(j, choice[j & 1], mask)) for j in range(devices)] for mask in range(1, size)
        ]
        return size, spot, perms

    for choice in rounds:
        size, spot, perms = plan(choice)
        piece = block.shape[0] // size
        total = lax.dynamic_slice_in_dim(block, spot * piece, piece, 0)
        for mask, perm in zip(range(1, size), perms):
            send = lax.dynamic_slice_in_dim(block, (spot ^ mask) * piece, piece, 0)
            got = lax.ppermute(send.astype(jnp.bfloat16), ("grp", "seq"), perm)
            total = total + got.astype(jnp.float32)
        block = total
    block = block.astype(jnp.bfloat16)
    for choice in reversed(rounds):
        size, spot, perms = plan(choice)
        piece = block.shape[0]
        whole = jnp.zeros((size * piece,) + block.shape[1:], block.dtype)
        whole = lax.dynamic_update_slice_in_dim(whole, block, spot * piece, 0)
        for mask, perm in zip(range(1, size), perms):
            got = lax.ppermute(block, ("grp", "seq"), perm)
            whole = lax.dynamic_update_slice_in_dim(whole, got, (spot ^ mask) * piece, 0)
        block = whole
    flat = block.reshape(-1).astype(jnp.float32)
    sums = []
    start = 0
    for part in parts:
        sums.append(flat[start : start + part.size].reshape(part.shape))
        start += part.size
    return tuple(sums)


def body(
    clip_latents, adjoint_seed, kernel_matrix, triple_projector, exit_projector, logit_scaling
):
    frames = clip_latents.shape[1]
    height = clip_latents.shape[2]
    channels = exit_projector.shape[0]
    breadth = clip_latents.shape[3] // channels
    places = height * breadth
    source = clip_latents.reshape(frames, height, breadth, channels)
    latent_features, patches, pull_act = spatial_forward(source, kernel_matrix)
    placed_features = lax.all_to_all(
        latent_features.reshape(frames, places, channels),
        "seq",
        split_axis=1,
        concat_axis=0,
        tiled=True,
    )
    section_outcome, standardised_tokens, mapped_tokens, softmax_blend = temporal_mixing_apply(
        placed_features, triple_projector, exit_projector, logit_scaling
    )
    output = lax.all_to_all(
        section_outcome, "seq", split_axis=0, concat_axis=1, tiled=True
    ).reshape(clip_latents.shape)
    upstream_adjoint = lax.all_to_all(
        adjoint_seed.reshape(frames, places, channels),
        "seq",
        split_axis=1,
        concat_axis=0,
        tiled=True,
    )
    feature_adjoint, triple_projector_adjoint, emitted_adjoint = temporal_mixing_reverse(
        placed_features,
        upstream_adjoint,
        standardised_tokens,
        mapped_tokens,
        softmax_blend,
        triple_projector,
        exit_projector,
        logit_scaling,
    )
    back_frames = lax.all_to_all(feature_adjoint, "seq", split_axis=0, concat_axis=1, tiled=True)
    d_source, grad_conv = spatial_backward(
        back_frames.reshape(frames * places, channels),
        patches,
        pull_act,
        kernel_matrix,
        frames,
        height,
        breadth,
    )
    d_video = d_source.reshape(clip_latents.shape)
    factor = 1.0 / math.sqrt(lax.axis_size("grp") * lax.axis_size("seq") * frames * places)
    g_conv_t, g_qkv, g_out = tree_all_reduce(
        (grad_conv.T * factor, triple_projector_adjoint * factor, emitted_adjoint * factor)
    )
    g_conv = g_conv_t.T
    return (output, d_video, g_conv, g_qkv, g_out)


def solution(mesh):
    return jax.shard_map(
        body,
        mesh=mesh,
        in_specs=(P("grp", "seq", None, None), P("grp", "seq", None, None), P(), P(), P(), P()),
        out_specs=(P("grp", "seq", None, None), P("grp", "seq", None, None), P(), P(), P()),
        check_vma=False,
    )
```

```python
import math

import jax
import jax.numpy as jnp
from jax import lax
from jax.sharding import PartitionSpec as P

HEAD_DIM = 64
GROUPS = 32


def group_act(widened):
    frames, height, breadth, channels = widened.shape
    span = channels // GROUPS
    count = height * breadth * span
    tokens = widened.reshape(frames, height * breadth, channels)

    def per_group(column_sums):
        totals = column_sums.reshape(frames, GROUPS, span).sum(axis=-1) / count
        return jnp.repeat(totals, span, axis=-1)[:, None, :]

    centre = per_group(jnp.sum(tokens, axis=1))
    shifted = tokens - centre
    spread = per_group(jnp.sum(jnp.square(shifted), axis=1))
    normed = shifted * lax.rsqrt(spread + 1e-05)
    return jax.nn.silu(normed).reshape(frames, height, breadth, channels)


def make_patches(active):
    frames, height, breadth, channels = active.shape
    padded = jnp.pad(active, ((0, 0), (1, 1), (1, 1), (0, 0)))
    pieces = [
        padded[:, down_step : down_step + height, side_step : side_step + breadth, :]
        for down_step in range(3)
        for side_step in range(3)
    ]
    return jnp.concatenate(pieces, axis=-1).reshape(frames * height * breadth, 9 * channels)


def fold_patches(columns, frames, height, breadth):
    channels = columns.shape[-1] // 9
    pieces = columns.reshape(frames, height, breadth, 9, channels)
    totals = jnp.zeros((frames, height + 2, breadth + 2, channels), jnp.float32)
    for down_step in range(3):
        for side_step in range(3):
            shifted = pieces[:, :, :, down_step * 3 + side_step, :]
            totals = totals + jnp.pad(
                shifted, ((0, 0), (down_step, 2 - down_step), (side_step, 2 - side_step), (0, 0))
            )
    return totals[:, 1 : height + 1, 1 : breadth + 1, :]


def layer_norm(widened):
    centre = jnp.mean(widened, axis=-1, keepdims=True)
    spread = jnp.mean(jnp.square(widened - centre), axis=-1, keepdims=True)
    return (widened - centre) * lax.rsqrt(spread + 1e-05)


def temporal_mixing(mapped_tokens, logit_scaling):
    frames, places, triple = mapped_tokens.shape
    channels = triple // 3
    head_count = channels // HEAD_DIM
    pieces = mapped_tokens.reshape(frames, places, 3, head_count, HEAD_DIM)
    query = pieces[:, :, 0]
    keys = pieces[:, :, 1]
    values = pieces[:, :, 2].astype(jnp.bfloat16)
    query = (
        query
        * lax.rsqrt(jnp.sum(query * query, axis=-1, keepdims=True) + 1e-06)
        * logit_scaling[:, None]
    ).astype(jnp.bfloat16)
    keys = (keys * lax.rsqrt(jnp.sum(keys * keys, axis=-1, keepdims=True) + 1e-06)).astype(
        jnp.bfloat16
    )
    scores = jnp.einsum("flhd,glhd->lhfg", query, keys, preferred_element_type=jnp.float32)
    weights = jnp.exp(scores)
    weights = (weights / jnp.sum(weights, axis=-1, keepdims=True)).astype(jnp.bfloat16)
    blend = jnp.einsum("lhfg,glhd->flhd", weights, values, preferred_element_type=jnp.float32)
    return blend.reshape(frames, places, channels)


def contract_rows(left, right):
    return lax.dot_general(
        left, right, (((0,), (0,)), ((), ())), preferred_element_type=jnp.float32
    )


def spatial_conv(tokens, kernel):
    return lax.conv_general_dilated(
        tokens,
        kernel,
        window_strides=(1, 1),
        padding=((1, 1), (1, 1)),
        dimension_numbers=("NHWC", "HWIO", "NHWC"),
        preferred_element_type=jnp.float32,
    )


def spatial_forward(source, kernel_matrix):
    frames, height, breadth, channels = source.shape
    widened = source.astype(jnp.float32)
    active, pull_act = jax.vjp(group_act, widened)
    active = active.astype(jnp.bfloat16)
    convolved = spatial_conv(active, kernel_matrix.reshape(3, 3, channels, channels))
    latent_features = (widened + convolved).astype(jnp.bfloat16)
    return (latent_features.reshape(frames * height * breadth, channels), active, pull_act)


def spatial_backward(upstream_adjoint, active, pull_act, kernel_matrix, frames, height, breadth):
    channels = upstream_adjoint.shape[-1]
    states_adjoint = upstream_adjoint.reshape(frames, height, breadth, channels)
    padded = jnp.pad(active, ((0, 0), (1, 1), (1, 1), (0, 0)))
    taps = lax.conv_general_dilated(
        padded,
        states_adjoint,
        window_strides=(1, 1),
        padding="VALID",
        dimension_numbers=("CHWN", "IHWO", "CHWN"),
        preferred_element_type=jnp.float32,
    )
    grad_conv = taps.reshape(channels, 9 * channels).T
    flipped = jnp.transpose(kernel_matrix.reshape(3, 3, channels, channels)[::-1, ::-1], (0, 1, 3, 2))
    d_active = spatial_conv(states_adjoint, flipped)
    d_source = pull_act(d_active)[0]
    section_outcome = (states_adjoint.astype(jnp.float32) + d_source).astype(jnp.bfloat16)
    return (section_outcome, grad_conv)


def temporal_mixing_apply(latent_features, triple_projector, exit_projector, logit_scaling):
    frames, places, channels = latent_features.shape
    widened = latent_features.astype(jnp.float32)
    standardised_tokens = layer_norm(widened).astype(jnp.bfloat16)
    mapped_tokens = jnp.dot(
        standardised_tokens.reshape(frames * places, channels),
        triple_projector,
        preferred_element_type=jnp.float32,
    ).reshape(frames, places, 3 * channels)
    softmax_blend = temporal_mixing(mapped_tokens, logit_scaling).astype(jnp.bfloat16)
    branch = jnp.dot(
        softmax_blend.reshape(frames * places, channels),
        exit_projector,
        preferred_element_type=jnp.float32,
    )
    section_outcome = (widened + branch.reshape(frames, places, channels)).astype(jnp.bfloat16)
    return (section_outcome, standardised_tokens, mapped_tokens, softmax_blend)


def temporal_mixing_reverse(
    latent_features,
    upstream_adjoint,
    standardised_tokens,
    mapped_tokens,
    softmax_blend,
    triple_projector,
    exit_projector,
    logit_scaling,
):
    frames, places, channels = latent_features.shape
    rows_cot = upstream_adjoint.reshape(frames * places, channels)
    emitted_adjoint = contract_rows(softmax_blend.reshape(frames * places, channels), rows_cot)
    d_mixture = jnp.dot(rows_cot, exit_projector.T, preferred_element_type=jnp.float32).astype(
        jnp.bfloat16
    )
    discarded_item, temporal_mixing_adjoint = jax.vjp(
        lambda entry_tensor: temporal_mixing(entry_tensor, logit_scaling), mapped_tokens
    )
    d_projected = temporal_mixing_adjoint(
        d_mixture.astype(jnp.float32).reshape(frames, places, channels)
    )[0].astype(jnp.bfloat16)
    rows_proj = d_projected.reshape(frames * places, 3 * channels)
    triple_projector_adjoint = contract_rows(
        standardised_tokens.reshape(frames * places, channels), rows_proj
    )
    d_normed = jnp.dot(rows_proj, triple_projector.T, preferred_element_type=jnp.float32).reshape(
        frames, places, channels
    )
    discarded_item, pull_norm = jax.vjp(layer_norm, latent_features.astype(jnp.float32))
    d_layer = pull_norm(d_normed)[0].astype(jnp.bfloat16)
    feature_adjoint = (upstream_adjoint.astype(jnp.float32) + d_layer.astype(jnp.float32)).astype(
        jnp.bfloat16
    )
    return (feature_adjoint, triple_projector_adjoint, emitted_adjoint)


CORE_BITS = (0,)
AXIS_BITS = {"x": (3, 6), "y": (4, 5), "z": (1, 2)}
ROUNDS = (("x", "z", "y"), ("z", "y", "x"))


def tree_all_reduce(parts):
    devices = lax.axis_size("grp") * lax.axis_size("seq")
    flat = jnp.concatenate([part.reshape(-1) for part in parts])
    rows = -(-flat.size // (devices * 128 * 8)) * 8
    flat = jnp.pad(flat, (0, devices * rows * 128 - flat.size))
    block = flat.reshape(devices, rows, 128)
    me = lax.axis_index("grp") * lax.axis_size("seq") + lax.axis_index("seq")
    core = me & 1
    rounds = [(CORE_BITS, CORE_BITS)] + [
        (AXIS_BITS[first], AXIS_BITS[second]) for first, second in zip(*ROUNDS)
    ]

    def flip(j, bits, mask):
        for place, bit in enumerate(bits):
            if (mask >> place) & 1:
                j ^= 1 << bit
        return j

    def position(bits):
        return sum(((me >> bit) & 1) << place for place, bit in enumerate(bits))

    def plan(choice):
        size = 1 << len(choice[0])
        spot = jnp.where(core == 0, position(choice[0]), position(choice[1]))
        perms = [
            [(j, flip(j, choice[j & 1], mask)) for j in range(devices)] for mask in range(1, size)
        ]
        return size, spot, perms

    for choice in rounds:
        size, spot, perms = plan(choice)
        piece = block.shape[0] // size
        total = lax.dynamic_slice_in_dim(block, spot * piece, piece, 0)
        for mask, perm in zip(range(1, size), perms):
            send = lax.dynamic_slice_in_dim(block, (spot ^ mask) * piece, piece, 0)
            got = lax.ppermute(send.astype(jnp.bfloat16), ("grp", "seq"), perm)
            total = total + got.astype(jnp.float32)
        block = total
    block = block.astype(jnp.bfloat16)
    for choice in reversed(rounds):
        size, spot, perms = plan(choice)
        piece = block.shape[0]
        whole = jnp.zeros((size * piece,) + block.shape[1:], block.dtype)
        whole = lax.dynamic_update_slice_in_dim(whole, block, spot * piece, 0)
        for mask, perm in zip(range(1, size), perms):
            got = lax.ppermute(block, ("grp", "seq"), perm)
            whole = lax.dynamic_update_slice_in_dim(whole, got, (spot ^ mask) * piece, 0)
        block = whole
    flat = block.reshape(-1).astype(jnp.float32)
    sums = []
    start = 0
    for part in parts:
        sums.append(flat[start : start + part.size].reshape(part.shape))
        start += part.size
    return tuple(sums)


def body(
    clip_latents, adjoint_seed, kernel_matrix, triple_projector, exit_projector, logit_scaling
):
    frames = clip_latents.shape[1]
    height = clip_latents.shape[2]
    channels = exit_projector.shape[0]
    breadth = clip_latents.shape[3] // channels
    places = height * breadth
    source = clip_latents.reshape(frames, height, breadth, channels)
    latent_features, patches, pull_act = spatial_forward(source, kernel_matrix)
    placed_features = lax.all_to_all(
        latent_features.reshape(frames, places, channels),
        "seq",
        split_axis=1,
        concat_axis=0,
        tiled=True,
    )
    section_outcome, standardised_tokens, mapped_tokens, softmax_blend = temporal_mixing_apply(
        placed_features, triple_projector, exit_projector, logit_scaling
    )
    output = lax.all_to_all(
        section_outcome, "seq", split_axis=0, concat_axis=1, tiled=True
    ).reshape(clip_latents.shape)
    upstream_adjoint = lax.all_to_all(
        adjoint_seed.reshape(frames, places, channels),
        "seq",
        split_axis=1,
        concat_axis=0,
        tiled=True,
    )
    feature_adjoint, triple_projector_adjoint, emitted_adjoint = temporal_mixing_reverse(
        placed_features,
        upstream_adjoint,
        standardised_tokens,
        mapped_tokens,
        softmax_blend,
        triple_projector,
        exit_projector,
        logit_scaling,
    )
    back_frames = lax.all_to_all(feature_adjoint, "seq", split_axis=0, concat_axis=1, tiled=True)
    d_source, grad_conv = spatial_backward(
        back_frames.reshape(frames * places, channels),
        patches,
        pull_act,
        kernel_matrix,
        frames,
        height,
        breadth,
    )
    d_video = d_source.reshape(clip_latents.shape)
    factor = 1.0 / math.sqrt(lax.axis_size("grp") * lax.axis_size("seq") * frames * places)
    g_conv_t, g_qkv, g_out = tree_all_reduce(
        (grad_conv.T * factor, triple_projector_adjoint * factor, emitted_adjoint * factor)
    )
    g_conv = g_conv_t.T
    return (output, d_video, g_conv, g_qkv, g_out)


def solution(mesh):
    return jax.shard_map(
        body,
        mesh=mesh,
        in_specs=(P("grp", "seq", None, None), P("grp", "seq", None, None), P(), P(), P(), P()),
        out_specs=(P("grp", "seq", None, None), P("grp", "seq", None, None), P(), P(), P()),
        check_vma=False,
    )
```

```python
import math

import jax
import jax.numpy as jnp
from jax import lax
from jax.sharding import PartitionSpec as P

HEAD_DIM = 64
GROUPS = 32


def group_act(widened):
    frames, height, breadth, channels = widened.shape
    span = channels // GROUPS
    count = height * breadth * span
    tokens = widened.reshape(frames, height * breadth, channels)

    def per_group(column_sums):
        totals = column_sums.reshape(frames, GROUPS, span).sum(axis=-1) / count
        return jnp.repeat(totals, span, axis=-1)[:, None, :]

    centre = per_group(jnp.sum(tokens, axis=1))
    shifted = tokens - centre
    spread = per_group(jnp.sum(jnp.square(shifted), axis=1))
    normed = shifted * lax.rsqrt(spread + 1e-05)
    return jax.nn.silu(normed).reshape(frames, height, breadth, channels)


def make_patches(active):
    frames, height, breadth, channels = active.shape
    padded = jnp.pad(active, ((0, 0), (1, 1), (1, 1), (0, 0)))
    pieces = [
        padded[:, down_step : down_step + height, side_step : side_step + breadth, :]
        for down_step in range(3)
        for side_step in range(3)
    ]
    return jnp.concatenate(pieces, axis=-1).reshape(frames * height * breadth, 9 * channels)


def fold_patches(columns, frames, height, breadth):
    channels = columns.shape[-1] // 9
    pieces = columns.reshape(frames, height, breadth, 9, channels)
    totals = jnp.zeros((frames, height + 2, breadth + 2, channels), jnp.float32)
    for down_step in range(3):
        for side_step in range(3):
            shifted = pieces[:, :, :, down_step * 3 + side_step, :]
            totals = totals + jnp.pad(
                shifted, ((0, 0), (down_step, 2 - down_step), (side_step, 2 - side_step), (0, 0))
            )
    return totals[:, 1 : height + 1, 1 : breadth + 1, :]


def layer_norm(widened):
    centre = jnp.mean(widened, axis=-1, keepdims=True)
    spread = jnp.mean(jnp.square(widened - centre), axis=-1, keepdims=True)
    return (widened - centre) * lax.rsqrt(spread + 1e-05)


def head_mixing(query, keys, values, scaling):
    query = (
        query * lax.rsqrt(jnp.sum(query * query, axis=-1, keepdims=True) + 1e-06) * scaling
    ).astype(jnp.bfloat16)
    keys = (keys * lax.rsqrt(jnp.sum(keys * keys, axis=-1, keepdims=True) + 1e-06)).astype(
        jnp.bfloat16
    )
    values = values.astype(jnp.bfloat16)
    scores = jnp.einsum("fld,gld->lfg", query, keys, preferred_element_type=jnp.float32)
    weights = jnp.exp(scores)
    weights = (weights / jnp.sum(weights, axis=-1, keepdims=True)).astype(jnp.bfloat16)
    return jnp.einsum("lfg,gld->fld", weights, values, preferred_element_type=jnp.float32)


def temporal_mixing(mapped_tokens, logit_scaling):
    frames, places, triple = mapped_tokens.shape
    channels = triple // 3
    head_count = channels // HEAD_DIM
    blends = []
    for head in range(head_count):
        low = head * HEAD_DIM
        blends.append(
            head_mixing(
                mapped_tokens[:, :, low : low + HEAD_DIM],
                mapped_tokens[:, :, channels + low : channels + low + HEAD_DIM],
                mapped_tokens[:, :, 2 * channels + low : 2 * channels + low + HEAD_DIM],
                logit_scaling[head],
            )
        )
    return jnp.concatenate(blends, axis=-1)


def contract_rows(left, right):
    return lax.dot_general(
        left, right, (((0,), (0,)), ((), ())), preferred_element_type=jnp.float32
    )


def spatial_conv(tokens, kernel):
    return lax.conv_general_dilated(
        tokens,
        kernel,
        window_strides=(1, 1),
        padding=((1, 1), (1, 1)),
        dimension_numbers=("NHWC", "HWIO", "NHWC"),
        preferred_element_type=jnp.float32,
    )


def spatial_forward(source, kernel_matrix):
    frames, height, breadth, channels = source.shape
    widened = source.astype(jnp.float32)
    active, pull_act = jax.vjp(group_act, widened)
    active = active.astype(jnp.bfloat16)
    convolved = spatial_conv(active, kernel_matrix.reshape(3, 3, channels, channels))
    latent_features = (widened + convolved).astype(jnp.bfloat16)
    return (latent_features.reshape(frames * height * breadth, channels), active, pull_act)


def spatial_backward(upstream_adjoint, active, pull_act, kernel_matrix, frames, height, breadth):
    channels = upstream_adjoint.shape[-1]
    states_adjoint = upstream_adjoint.reshape(frames, height, breadth, channels)
    padded = jnp.pad(active, ((0, 0), (1, 1), (1, 1), (0, 0)))
    taps = lax.conv_general_dilated(
        padded,
        states_adjoint,
        window_strides=(1, 1),
        padding="VALID",
        dimension_numbers=("CHWN", "IHWO", "NHWC"),
        preferred_element_type=jnp.float32,
    )
    grad_conv = jnp.transpose(taps, (1, 2, 0, 3)).reshape(9 * channels, channels)
    flipped = jnp.transpose(kernel_matrix.reshape(3, 3, channels, channels)[::-1, ::-1], (0, 1, 3, 2))
    d_active = spatial_conv(states_adjoint, flipped)
    d_source = pull_act(d_active)[0]
    section_outcome = (states_adjoint.astype(jnp.float32) + d_source).astype(jnp.bfloat16)
    return (section_outcome, grad_conv)


def temporal_mixing_apply(latent_features, triple_projector, exit_projector, logit_scaling):
    frames, places, channels = latent_features.shape
    widened = latent_features.astype(jnp.float32)
    standardised_tokens = layer_norm(widened).astype(jnp.bfloat16)
    mapped_tokens = jnp.dot(
        standardised_tokens.reshape(frames * places, channels),
        triple_projector,
        preferred_element_type=jnp.float32,
    ).reshape(frames, places, 3 * channels)
    softmax_blend = temporal_mixing(mapped_tokens, logit_scaling).astype(jnp.bfloat16)
    branch = jnp.dot(
        softmax_blend.reshape(frames * places, channels),
        exit_projector,
        preferred_element_type=jnp.float32,
    )
    section_outcome = (widened + branch.reshape(frames, places, channels)).astype(jnp.bfloat16)
    return (section_outcome, standardised_tokens, mapped_tokens, softmax_blend)


def temporal_mixing_reverse(
    latent_features,
    upstream_adjoint,
    standardised_tokens,
    mapped_tokens,
    softmax_blend,
    triple_projector,
    exit_projector,
    logit_scaling,
):
    frames, places, channels = latent_features.shape
    rows_cot = upstream_adjoint.reshape(frames * places, channels)
    emitted_adjoint = contract_rows(softmax_blend.reshape(frames * places, channels), rows_cot)
    d_mixture = jnp.dot(rows_cot, exit_projector.T, preferred_element_type=jnp.float32).astype(
        jnp.bfloat16
    )
    discarded_item, temporal_mixing_adjoint = jax.vjp(
        lambda entry_tensor: temporal_mixing(entry_tensor, logit_scaling), mapped_tokens
    )
    d_projected = temporal_mixing_adjoint(
        d_mixture.astype(jnp.float32).reshape(frames, places, channels)
    )[0].astype(jnp.bfloat16)
    rows_proj = d_projected.reshape(frames * places, 3 * channels)
    triple_projector_adjoint = contract_rows(
        standardised_tokens.reshape(frames * places, channels), rows_proj
    )
    d_normed = jnp.dot(rows_proj, triple_projector.T, preferred_element_type=jnp.float32).reshape(
        frames, places, channels
    )
    discarded_item, pull_norm = jax.vjp(layer_norm, latent_features.astype(jnp.float32))
    d_layer = pull_norm(d_normed)[0].astype(jnp.bfloat16)
    feature_adjoint = (upstream_adjoint.astype(jnp.float32) + d_layer.astype(jnp.float32)).astype(
        jnp.bfloat16
    )
    return (feature_adjoint, triple_projector_adjoint, emitted_adjoint)


CORE_BITS = (0,)
AXIS_BITS = {"x": (3, 6), "y": (4, 5), "z": (1, 2)}
ROUNDS = (("x", "z", "y"), ("z", "y", "x"))


def tree_all_reduce(parts):
    devices = lax.axis_size("grp") * lax.axis_size("seq")
    flat = jnp.concatenate([part.reshape(-1) for part in parts])
    rows = -(-flat.size // (devices * 128 * 8)) * 8
    flat = jnp.pad(flat, (0, devices * rows * 128 - flat.size))
    block = flat.reshape(devices, rows, 128)
    me = lax.axis_index("grp") * lax.axis_size("seq") + lax.axis_index("seq")
    core = me & 1
    rounds = [(CORE_BITS, CORE_BITS)] + [
        (AXIS_BITS[first], AXIS_BITS[second]) for first, second in zip(*ROUNDS)
    ]

    def flip(j, bits, mask):
        for place, bit in enumerate(bits):
            if (mask >> place) & 1:
                j ^= 1 << bit
        return j

    def position(bits):
        return sum(((me >> bit) & 1) << place for place, bit in enumerate(bits))

    def plan(choice):
        size = 1 << len(choice[0])
        spot = jnp.where(core == 0, position(choice[0]), position(choice[1]))
        perms = [
            [(j, flip(j, choice[j & 1], mask)) for j in range(devices)] for mask in range(1, size)
        ]
        return size, spot, perms

    for choice in rounds:
        size, spot, perms = plan(choice)
        piece = block.shape[0] // size
        total = lax.dynamic_slice_in_dim(block, spot * piece, piece, 0)
        for mask, perm in zip(range(1, size), perms):
            send = lax.dynamic_slice_in_dim(block, (spot ^ mask) * piece, piece, 0)
            got = lax.ppermute(send.astype(jnp.bfloat16), ("grp", "seq"), perm)
            total = total + got.astype(jnp.float32)
        block = total
    block = block.astype(jnp.bfloat16)
    for choice in reversed(rounds):
        size, spot, perms = plan(choice)
        piece = block.shape[0]
        whole = jnp.zeros((size * piece,) + block.shape[1:], block.dtype)
        whole = lax.dynamic_update_slice_in_dim(whole, block, spot * piece, 0)
        for mask, perm in zip(range(1, size), perms):
            got = lax.ppermute(block, ("grp", "seq"), perm)
            whole = lax.dynamic_update_slice_in_dim(whole, got, (spot ^ mask) * piece, 0)
        block = whole
    flat = block.reshape(-1).astype(jnp.float32)
    sums = []
    start = 0
    for part in parts:
        sums.append(flat[start : start + part.size].reshape(part.shape))
        start += part.size
    return tuple(sums)


def body(
    clip_latents, adjoint_seed, kernel_matrix, triple_projector, exit_projector, logit_scaling
):
    frames = clip_latents.shape[1]
    height = clip_latents.shape[2]
    channels = exit_projector.shape[0]
    breadth = clip_latents.shape[3] // channels
    places = height * breadth
    source = clip_latents.reshape(frames, height, breadth, channels)
    latent_features, patches, pull_act = spatial_forward(source, kernel_matrix)
    placed_features = lax.all_to_all(
        latent_features.reshape(frames, places, channels),
        "seq",
        split_axis=1,
        concat_axis=0,
        tiled=True,
    )
    section_outcome, standardised_tokens, mapped_tokens, softmax_blend = temporal_mixing_apply(
        placed_features, triple_projector, exit_projector, logit_scaling
    )
    output = lax.all_to_all(
        section_outcome, "seq", split_axis=0, concat_axis=1, tiled=True
    ).reshape(clip_latents.shape)
    upstream_adjoint = lax.all_to_all(
        adjoint_seed.reshape(frames, places, channels),
        "seq",
        split_axis=1,
        concat_axis=0,
        tiled=True,
    )
    feature_adjoint, triple_projector_adjoint, emitted_adjoint = temporal_mixing_reverse(
        placed_features,
        upstream_adjoint,
        standardised_tokens,
        mapped_tokens,
        softmax_blend,
        triple_projector,
        exit_projector,
        logit_scaling,
    )
    back_frames = lax.all_to_all(feature_adjoint, "seq", split_axis=0, concat_axis=1, tiled=True)
    d_source, grad_conv = spatial_backward(
        back_frames.reshape(frames * places, channels),
        patches,
        pull_act,
        kernel_matrix,
        frames,
        height,
        breadth,
    )
    d_video = d_source.reshape(clip_latents.shape)
    factor = 1.0 / math.sqrt(lax.axis_size("grp") * lax.axis_size("seq") * frames * places)
    g_conv_t, g_qkv, g_out = tree_all_reduce(
        (grad_conv.T * factor, triple_projector_adjoint * factor, emitted_adjoint * factor)
    )
    g_conv = g_conv_t.T
    return (output, d_video, g_conv, g_qkv, g_out)


def solution(mesh):
    return jax.shard_map(
        body,
        mesh=mesh,
        in_specs=(P("grp", "seq", None, None), P("grp", "seq", None, None), P(), P(), P(), P()),
        out_specs=(P("grp", "seq", None, None), P("grp", "seq", None, None), P(), P(), P()),
        check_vma=False,
    )
```

```python
import math

import jax
import jax.numpy as jnp
from jax import lax
from jax.sharding import PartitionSpec as P

HEAD_DIM = 64
GROUPS = 32


def group_act(widened):
    frames, height, breadth, channels = widened.shape
    span = channels // GROUPS
    count = height * breadth * span
    tokens = widened.reshape(frames, height * breadth, channels)

    def per_group(column_sums):
        totals = column_sums.reshape(frames, GROUPS, span).sum(axis=-1) / count
        return jnp.repeat(totals, span, axis=-1)[:, None, :]

    centre = per_group(jnp.sum(tokens, axis=1))
    shifted = tokens - centre
    spread = per_group(jnp.sum(jnp.square(shifted), axis=1))
    normed = shifted * lax.rsqrt(spread + 1e-05)
    return jax.nn.silu(normed).reshape(frames, height, breadth, channels)


def make_patches(active):
    frames, height, breadth, channels = active.shape
    padded = jnp.pad(active, ((0, 0), (1, 1), (1, 1), (0, 0)))
    pieces = [
        padded[:, down_step : down_step + height, side_step : side_step + breadth, :]
        for down_step in range(3)
        for side_step in range(3)
    ]
    return jnp.concatenate(pieces, axis=-1).reshape(frames * height * breadth, 9 * channels)


def fold_patches(columns, frames, height, breadth):
    channels = columns.shape[-1] // 9
    pieces = columns.reshape(frames, height, breadth, 9, channels)
    totals = jnp.zeros((frames, height + 2, breadth + 2, channels), jnp.float32)
    for down_step in range(3):
        for side_step in range(3):
            shifted = pieces[:, :, :, down_step * 3 + side_step, :]
            totals = totals + jnp.pad(
                shifted, ((0, 0), (down_step, 2 - down_step), (side_step, 2 - side_step), (0, 0))
            )
    return totals[:, 1 : height + 1, 1 : breadth + 1, :]


def layer_norm(widened):
    centre = jnp.mean(widened, axis=-1, keepdims=True)
    spread = jnp.mean(jnp.square(widened - centre), axis=-1, keepdims=True)
    return (widened - centre) * lax.rsqrt(spread + 1e-05)


def temporal_mixing(mapped_tokens, logit_scaling):
    frames, places, triple = mapped_tokens.shape
    channels = triple // 3
    head_count = channels // HEAD_DIM
    pieces = mapped_tokens.reshape(frames, places, 3, head_count, HEAD_DIM)
    query = pieces[:, :, 0]
    keys = pieces[:, :, 1]
    values = pieces[:, :, 2].astype(jnp.bfloat16)
    query = (
        query
        * lax.rsqrt(jnp.sum(query * query, axis=-1, keepdims=True) + 1e-06)
        * logit_scaling[:, None]
    ).astype(jnp.bfloat16)
    keys = (keys * lax.rsqrt(jnp.sum(keys * keys, axis=-1, keepdims=True) + 1e-06)).astype(
        jnp.bfloat16
    )
    scores = jnp.einsum("flhd,glhd->lhfg", query, keys, preferred_element_type=jnp.float32)
    weights = jnp.exp(scores)
    weights = (weights / jnp.sum(weights, axis=-1, keepdims=True)).astype(jnp.bfloat16)
    blend = jnp.einsum("lhfg,glhd->flhd", weights, values, preferred_element_type=jnp.float32)
    return blend.reshape(frames, places, channels)


def contract_rows(left, right):
    return lax.dot_general(
        left, right, (((0,), (0,)), ((), ())), preferred_element_type=jnp.float32
    )


def spatial_conv(tokens, kernel):
    return lax.conv_general_dilated(
        tokens,
        kernel,
        window_strides=(1, 1),
        padding=((1, 1), (1, 1)),
        dimension_numbers=("NHWC", "HWIO", "NHWC"),
        preferred_element_type=jnp.float32,
    )


def spatial_forward(source, kernel_matrix):
    frames, height, breadth, channels = source.shape
    widened = source.astype(jnp.float32)
    active, pull_act = jax.vjp(group_act, widened)
    active = active.astype(jnp.bfloat16)
    convolved = spatial_conv(active, kernel_matrix.reshape(3, 3, channels, channels))
    latent_features = (widened + convolved).astype(jnp.bfloat16)
    return (latent_features.reshape(frames * height * breadth, channels), active, pull_act)


def spatial_backward(upstream_adjoint, active, pull_act, kernel_matrix, frames, height, breadth):
    channels = upstream_adjoint.shape[-1]
    states_adjoint = upstream_adjoint.reshape(frames, height, breadth, channels)
    padded = jnp.pad(active, ((0, 0), (1, 1), (1, 1), (0, 0)))
    taps = lax.conv_general_dilated(
        padded,
        states_adjoint,
        window_strides=(1, 1),
        padding="VALID",
        dimension_numbers=("CHWN", "IHWO", "NHWC"),
        preferred_element_type=jnp.float32,
    )
    grad_conv = jnp.transpose(taps, (1, 2, 0, 3)).reshape(9 * channels, channels)
    flipped = jnp.transpose(kernel_matrix.reshape(3, 3, channels, channels)[::-1, ::-1], (0, 1, 3, 2))
    d_active = spatial_conv(states_adjoint, flipped)
    d_source = pull_act(d_active)[0]
    section_outcome = (states_adjoint.astype(jnp.float32) + d_source).astype(jnp.bfloat16)
    return (section_outcome, grad_conv)


def temporal_mixing_apply(latent_features, triple_projector, exit_projector, logit_scaling):
    frames, places, channels = latent_features.shape
    widened = latent_features.astype(jnp.float32)
    standardised_tokens = layer_norm(widened).astype(jnp.bfloat16)
    mapped_tokens = jnp.dot(
        standardised_tokens.reshape(frames * places, channels),
        triple_projector,
        preferred_element_type=jnp.float32,
    ).reshape(frames, places, 3 * channels)
    softmax_blend = temporal_mixing(mapped_tokens, logit_scaling).astype(jnp.bfloat16)
    branch = jnp.dot(
        softmax_blend.reshape(frames * places, channels),
        exit_projector,
        preferred_element_type=jnp.float32,
    )
    section_outcome = (widened + branch.reshape(frames, places, channels)).astype(jnp.bfloat16)
    return (section_outcome, standardised_tokens, mapped_tokens, softmax_blend)


def temporal_mixing_reverse(
    latent_features,
    upstream_adjoint,
    standardised_tokens,
    mapped_tokens,
    softmax_blend,
    triple_projector,
    exit_projector,
    logit_scaling,
):
    frames, places, channels = latent_features.shape
    rows_cot = upstream_adjoint.reshape(frames * places, channels)
    emitted_adjoint = contract_rows(softmax_blend.reshape(frames * places, channels), rows_cot)
    d_mixture = jnp.dot(rows_cot, exit_projector.T, preferred_element_type=jnp.float32).astype(
        jnp.bfloat16
    )
    discarded_item, temporal_mixing_adjoint = jax.vjp(
        lambda entry_tensor: temporal_mixing(entry_tensor, logit_scaling), mapped_tokens
    )
    d_projected = temporal_mixing_adjoint(
        d_mixture.astype(jnp.float32).reshape(frames, places, channels)
    )[0].astype(jnp.bfloat16)
    rows_proj = d_projected.reshape(frames * places, 3 * channels)
    triple_projector_adjoint = contract_rows(
        standardised_tokens.reshape(frames * places, channels), rows_proj
    )
    d_normed = jnp.dot(rows_proj, triple_projector.T, preferred_element_type=jnp.float32).reshape(
        frames, places, channels
    )
    discarded_item, pull_norm = jax.vjp(layer_norm, latent_features.astype(jnp.float32))
    d_layer = pull_norm(d_normed)[0].astype(jnp.bfloat16)
    feature_adjoint = (upstream_adjoint.astype(jnp.float32) + d_layer.astype(jnp.float32)).astype(
        jnp.bfloat16
    )
    return (feature_adjoint, triple_projector_adjoint, emitted_adjoint)


CORE_BITS = (0,)
AXIS_BITS = {"x": (3, 6), "y": (4, 5), "z": (1, 2)}
ROUNDS = (("x", "z", "y"), ("z", "y", "x"))


def tree_all_reduce(parts):
    devices = lax.axis_size("grp") * lax.axis_size("seq")
    flat = jnp.concatenate([part.reshape(-1) for part in parts])
    rows = -(-flat.size // (devices * 128 * 8)) * 8
    flat = jnp.pad(flat, (0, devices * rows * 128 - flat.size))
    block = flat.reshape(devices, rows, 128)
    me = lax.axis_index("grp") * lax.axis_size("seq") + lax.axis_index("seq")
    core = me & 1
    rounds = [(CORE_BITS, CORE_BITS)] + [
        (AXIS_BITS[first], AXIS_BITS[second]) for first, second in zip(*ROUNDS)
    ]

    def flip(j, bits, mask):
        for place, bit in enumerate(bits):
            if (mask >> place) & 1:
                j ^= 1 << bit
        return j

    def position(bits):
        return sum(((me >> bit) & 1) << place for place, bit in enumerate(bits))

    def plan(choice):
        size = 1 << len(choice[0])
        spot = jnp.where(core == 0, position(choice[0]), position(choice[1]))
        perms = [
            [(j, flip(j, choice[j & 1], mask)) for j in range(devices)] for mask in range(1, size)
        ]
        return size, spot, perms

    for choice in rounds:
        size, spot, perms = plan(choice)
        piece = block.shape[0] // size
        total = lax.dynamic_slice_in_dim(block, spot * piece, piece, 0)
        for mask, perm in zip(range(1, size), perms):
            send = lax.dynamic_slice_in_dim(block, (spot ^ mask) * piece, piece, 0)
            got = lax.ppermute(send.astype(jnp.bfloat16), ("grp", "seq"), perm)
            total = total + got.astype(jnp.float32)
        block = total
    block = block.astype(jnp.bfloat16)
    for choice in reversed(rounds):
        size, spot, perms = plan(choice)
        piece = block.shape[0]
        whole = jnp.zeros((size * piece,) + block.shape[1:], block.dtype)
        whole = lax.dynamic_update_slice_in_dim(whole, block, spot * piece, 0)
        for mask, perm in zip(range(1, size), perms):
            got = lax.ppermute(block, ("grp", "seq"), perm)
            whole = lax.dynamic_update_slice_in_dim(whole, got, (spot ^ mask) * piece, 0)
        block = whole
    flat = block.reshape(-1).astype(jnp.float32)
    sums = []
    start = 0
    for part in parts:
        sums.append(flat[start : start + part.size].reshape(part.shape))
        start += part.size
    return tuple(sums)


def body(
    clip_latents, adjoint_seed, kernel_matrix, triple_projector, exit_projector, logit_scaling
):
    frames = clip_latents.shape[1]
    height = clip_latents.shape[2]
    channels = exit_projector.shape[0]
    breadth = clip_latents.shape[3] // channels
    places = height * breadth
    source = clip_latents.reshape(frames, height, breadth, channels)
    latent_features, patches, pull_act = spatial_forward(source, kernel_matrix)
    placed_features = lax.all_to_all(
        latent_features.reshape(frames, places, channels),
        "seq",
        split_axis=1,
        concat_axis=0,
        tiled=True,
    )
    section_outcome, standardised_tokens, mapped_tokens, softmax_blend = temporal_mixing_apply(
        placed_features, triple_projector, exit_projector, logit_scaling
    )
    output = lax.all_to_all(
        section_outcome, "seq", split_axis=0, concat_axis=1, tiled=True
    ).reshape(clip_latents.shape)
    upstream_adjoint = lax.all_to_all(
        adjoint_seed.reshape(frames, places, channels),
        "seq",
        split_axis=1,
        concat_axis=0,
        tiled=True,
    )
    feature_adjoint, triple_projector_adjoint, emitted_adjoint = temporal_mixing_reverse(
        placed_features,
        upstream_adjoint,
        standardised_tokens,
        mapped_tokens,
        softmax_blend,
        triple_projector,
        exit_projector,
        logit_scaling,
    )
    back_frames = lax.all_to_all(feature_adjoint, "seq", split_axis=0, concat_axis=1, tiled=True)
    d_source, grad_conv = spatial_backward(
        back_frames.reshape(frames * places, channels),
        patches,
        pull_act,
        kernel_matrix,
        frames,
        height,
        breadth,
    )
    d_video = d_source.reshape(clip_latents.shape)
    factor = 1.0 / math.sqrt(lax.axis_size("grp") * lax.axis_size("seq") * frames * places)
    g_conv, g_qkv, g_out = tree_all_reduce(
        (grad_conv * factor, triple_projector_adjoint * factor, emitted_adjoint * factor)
    )
    return (output, d_video, g_conv, g_qkv, g_out)


def solution(mesh):
    return jax.shard_map(
        body,
        mesh=mesh,
        in_specs=(P("grp", "seq", None, None), P("grp", "seq", None, None), P(), P(), P(), P()),
        out_specs=(P("grp", "seq", None, None), P("grp", "seq", None, None), P(), P(), P()),
        check_vma=False,
    )
```
